32 devices in a mesh: expert: 2 (over y), hidden: 16 (over z, x, core).
Axes of the slice: x: 2, y: 2, z: 4, core: 2. Of those that a mesh axis runs over, the one named last changes fastest.
Arguments:
- tokens: bfloat16 [192, 3072], P('expert', 'hidden'), may hold values from -6 to 6
- cotangent: bfloat16 [192, 3072], P('expert', 'hidden'), may hold values from -6 to 6
- w_gate: bfloat16 [2, 3072, 16384], P('expert', None, 'hidden'), may hold values from -0.15625 to 0.15625
- w_up: bfloat16 [2, 3072, 16384], P('expert', None, 'hidden'), may hold values from -0.15625 to 0.15625
- w_down: bfloat16 [2, 16384, 3072], P('expert', 'hidden'), may hold values from -0.046875 to 0.046875
- slot_token: int32 [2, 192], P(None, 'expert'), may hold values from 0 to 95, as said below
- slot_weight: float32 [2, 192], P(None, 'expert'), may hold values from 0.2 to 1
- keep_mask: int32 [2, 192, 16384], P('expert', None, 'hidden'), may hold values 0 or 1
Outputs:
- grad_tokens: bfloat16 [192, 3072], P('expert', 'hidden')
The draws below stay inside these ranges and needn't reach their ends.
Inputs may be any that keep to these rules, and one draw needn't show every extreme that they name: `slot_token`: slots s of block g = s // 96 of every expert hold tokens of group g (token rows g * 96 to (g + 1) * 96 - 1); within one expert and one block the 96 entries are distinct; every slot is filled.
All inputs are finite; a program needn't handle non-finite values. No bound on the sum of `keep_mask` on one device may be relied on, other than what follows from the above.
Results may differ from the reference program's by a relative error of at most 0.012.
Values may be sent and summed in bfloat16 or wider, within the bound.
No kernel may reach another device: no remote copies, remote signals or barrier semaphores. Data moves between devices by JAX's collectives and lax.ppermute only.
A program may use at most 64 MiB of HBM per device.

```python
import jax
import jax.numpy as jnp
from jax import lax

D = 3072
FF = 16384
C = 192
EXPERTS = 2
SRC_SLOTS = 96
TOK_G = 96
TOKENS = 192
N_EXPERT = 2


def draw_slot_token(key, part):
    block_keys = jax.random.split(key, EXPERTS * N_EXPERT)

    def one_block(block_key):
        return jax.random.permutation(block_key, TOK_G)[:SRC_SLOTS].astype(jnp.int32)
    blocks = jax.vmap(one_block)(block_keys)
    return blocks.reshape(EXPERTS, N_EXPERT * SRC_SLOTS)


def place_ends(array, rng, least, top_value):
    spot = [jax.random.randint(jax.random.fold_in(rng, axis), (), 0, length) for axis, length in enumerate(array.shape)]
    widest = array.shape.index(max(array.shape))
    next_to = spot[:widest] + [(spot[widest] + 1) % array.shape[widest]] + spot[widest + 1:]
    return array.at[tuple(spot)].set(least).at[tuple(next_to)].set(top_value)


def raised(entries, own_key, source, target, shards_of, factor):
    def block_of(position):
        return (jnp.arange(entries.shape[position]) // (entries.shape[position] // shards_of)).reshape((-1,) + (1,) * (entries.ndim - 1 - position))

    one_side = jax.random.permutation(own_key, shards_of)[block_of(target)]
    other_side = (block_of(target) + shards_of // 2) % shards_of
    return jnp.where((block_of(source) == one_side) | (block_of(source) == other_side), factor * entries, entries)


def level_of(key, shape, cuts, smallest, high):
    def one(dim, blocks):
        heights = jax.random.uniform(jax.random.fold_in(jax.random.fold_in(key, 6), dim), (blocks,), jnp.float32, smallest / len(cuts), high / len(cuts))
        return jnp.repeat(jnp.exp(heights), shape[dim] // blocks).reshape((-1,) + (1,) * (len(shape) - dim - 1))

    level = one(*cuts[0])
    for cut in cuts[1:]:
        level = level * one(*cut)
    return level


def noise(stream_key, shape, scale, bound, cuts=(), held_as=jnp.bfloat16):
    array = scale * jax.random.normal(stream_key, shape, jnp.float32)
    if cuts:
        array = array * level_of(stream_key, shape, cuts, -0.22, 0.18)
    return jnp.clip(array, -bound, bound).astype(held_as)


def noise_with(stream_key, extent, deviation, limit, cuts, heavy, kind=jnp.bfloat16):
    values = deviation * jax.random.normal(stream_key, extent, jnp.float32)
    if cuts:
        values = values * level_of(stream_key, extent, cuts, -0.22, 0.18)
    return jnp.clip(raised(values, jax.random.fold_in(stream_key, 3), *heavy), -limit, limit).astype(kind)


def setup_inputs(seed: int = 0) -> dict:
    arg_keys = jax.random.split(jax.random.key(seed), 9)
    tokens = noise(arg_keys[0], (TOKENS, D), 1.0, 6.0, ((0, 2), (1, 16)))
    cotangent = noise(arg_keys[1], (TOKENS, D), 1.0, 6.0, ((0, 2), (1, 16)))
    w_gate = noise_with(arg_keys[2], (EXPERTS, D, FF), D ** -0.5, 0.15625, ((0, 2), (2, 16)), (2, 1, 16, 2.0))
    w_up = noise_with(arg_keys[3], (EXPERTS, D, FF), D ** -0.5, 0.15625, ((0, 2), (2, 16)), (2, 1, 16, 2.0))
    w_down = noise(arg_keys[4], (EXPERTS, FF, D), FF ** -0.5, 0.046875, ((0, 2), (1, 16)))
    slot_token = draw_slot_token(jax.random.fold_in(arg_keys[8], 71), 0)
    slot_weight = jnp.clip(0.2 + 0.8 * jax.random.uniform(arg_keys[6], (EXPERTS, C), jnp.float32) ** level_of(arg_keys[6], (EXPERTS, C), ((1, 2),), -0.2, 0.2), 0.2, 1.0)
    keep_mask = place_ends((jax.random.randint(arg_keys[7], (EXPERTS, C, FF), 0, 10) < 9).astype(jnp.int32), jax.random.fold_in(arg_keys[7], 1), 0, 1)
    return dict(tokens=tokens, cotangent=cotangent, w_gate=w_gate, w_up=w_up, w_down=w_down, slot_token=slot_token, slot_weight=slot_weight, keep_mask=keep_mask)


keep_rate = 0.9

def gelu_tanh(values):
    return jax.nn.gelu(values, approximate=True)

def reference(tokens, cotangent, w_gate, w_up, w_down, slot_token, slot_weight, keep_mask):
    offsets = jnp.arange(C, dtype=jnp.int32) // SRC_SLOTS * TOK_G
    slot_rows = (slot_token.astype(jnp.int32) + offsets[None, :]).astype(jnp.int32)
    inv_keep = 1.0 / keep_rate

    def expert_step(totals, packed):
        token_rows, weights, gate_mat, up_mat, down_mat, mask_bits = packed
        slot_inputs = tokens[token_rows]
        slot_cot = (weights[:, None] * cotangent[token_rows].astype(jnp.float32)).astype(jnp.bfloat16)
        gate_pre = jnp.dot(slot_inputs, gate_mat, preferred_element_type=jnp.float32)
        up_pre = jnp.dot(slot_inputs, up_mat, preferred_element_type=jnp.float32)
        grad_hidden = lax.dot_general(slot_cot, down_mat, (((1,), (1,)), ((), ())), preferred_element_type=jnp.float32)
        activated, pullback = jax.vjp(gelu_tanh, gate_pre)
        grad_pre = grad_hidden * mask_bits.astype(jnp.float32) * inv_keep
        grad_up = (grad_pre * activated).astype(jnp.bfloat16)
        grad_gate = pullback(grad_pre * up_pre)[0].astype(jnp.bfloat16)
        slot_grad = lax.dot_general(grad_gate, gate_mat, (((1,), (1,)), ((), ())), preferred_element_type=jnp.float32)
        slot_grad = slot_grad + lax.dot_general(grad_up, up_mat, (((1,), (1,)), ((), ())), preferred_element_type=jnp.float32)
        totals = totals + jax.ops.segment_sum(slot_grad, token_rows, num_segments=TOKENS)
        return (totals, None)
    start_total = jnp.zeros((TOKENS, D), jnp.float32)
    totals, _ = lax.scan(expert_step, start_total, (slot_rows, slot_weight, w_gate, w_up, w_down, keep_mask))
    return totals.astype(jnp.bfloat16)
```

```python
import jax
import jax.numpy as jnp
from jax import lax
from jax.sharding import PartitionSpec as P

keep_rate = 0.9


def gelu_tanh(values):
    return jax.nn.gelu(values, approximate=True)


def fold_slots(one_hot, slot_values):
    high_part = slot_values.astype(jnp.bfloat16)
    low_part = (slot_values - high_part.astype(jnp.float32)).astype(jnp.bfloat16)
    dims = (((0,), (0,)), ((), ()))
    return lax.dot_general(one_hot, high_part, dims, preferred_element_type=jnp.float32) + lax.dot_general(
        one_hot, low_part, dims, preferred_element_type=jnp.float32
    )


def body(tokens, cotangent, w_gate, w_up, w_down, slot_token, slot_weight, keep_mask):
    gate_mat = w_gate[0]
    up_mat = w_up[0]
    down_mat = w_down[0]
    model_width, local_ff = gate_mat.shape
    hidden_count = lax.axis_size("hidden")
    expert_count = lax.axis_size("expert")
    expert_total, per_source = slot_token.shape
    slot_count = expert_count * per_source
    group_tokens, local_width = tokens.shape
    slot_list = slot_token.reshape(-1)
    weight_column = slot_weight.reshape(-1, 1)
    inv_keep = 1.0 / keep_rate

    chosen = tokens[slot_list]
    scaled = (weight_column * cotangent[slot_list].astype(jnp.float32)).astype(jnp.bfloat16)
    slab = jnp.concatenate([chosen, scaled], axis=1).reshape(expert_total, per_source, 2 * local_width)
    recv = lax.all_to_all(slab, "expert", split_axis=0, concat_axis=0, tiled=True)
    slab_slots = recv.reshape(slot_count, 2 * local_width)
    gathered = lax.all_gather(slab_slots, "hidden", axis=0, tiled=False)
    part_inputs = gathered[:, :, :local_width]
    part_cot = gathered[:, :, local_width:]

    gate_rows = gate_mat.reshape(hidden_count, local_width, local_ff)
    up_rows = up_mat.reshape(hidden_count, local_width, local_ff)
    down_cols = down_mat.reshape(local_ff, hidden_count, local_width)
    fwd_dims = (((0, 2), (0, 1)), ((), ()))
    gate_pre = lax.dot_general(part_inputs, gate_rows, fwd_dims, preferred_element_type=jnp.float32)
    up_pre = lax.dot_general(part_inputs, up_rows, fwd_dims, preferred_element_type=jnp.float32)
    grad_hidden = lax.dot_general(
        part_cot, down_cols, (((0, 2), (1, 2)), ((), ())), preferred_element_type=jnp.float32
    )
    activated, pullback = jax.vjp(gelu_tanh, gate_pre)
    grad_pre = grad_hidden * keep_mask[0].astype(jnp.float32) * inv_keep
    grad_up = (grad_pre * activated).astype(jnp.bfloat16)
    grad_gate = pullback(grad_pre * up_pre)[0].astype(jnp.bfloat16)

    back_dims = (((1,), (1,)), ((), ()))
    partial = lax.dot_general(
        grad_gate, gate_mat, back_dims, preferred_element_type=jnp.float32
    ) + lax.dot_general(grad_up, up_mat, back_dims, preferred_element_type=jnp.float32)
    blocks = partial.reshape(expert_count, per_source, hidden_count, local_width).transpose(0, 2, 1, 3)
    blocks = blocks.astype(jnp.bfloat16).reshape(expert_count * hidden_count, per_source, local_width)
    returned = lax.all_to_all(blocks, ("expert", "hidden"), split_axis=0, concat_axis=0, tiled=True)
    per_expert = returned.reshape(expert_total, hidden_count, per_source, local_width).astype(jnp.float32).sum(1)
    one_hot = (slot_list[:, None] == jnp.arange(group_tokens, dtype=jnp.int32)[None, :]).astype(jnp.bfloat16)
    token_sum = fold_slots(one_hot, per_expert.reshape(expert_total * per_source, local_width))
    return token_sum.astype(jnp.bfloat16)


def solution(mesh):
    in_specs = (
        P("expert", "hidden"),
        P("expert", "hidden"),
        P("expert", None, "hidden"),
        P("expert", None, "hidden"),
        P("expert", "hidden", None),
        P(None, "expert"),
        P(None, "expert"),
        P("expert", None, "hidden"),
    )
    out_specs = P("expert", "hidden")
    return jax.shard_map(body, mesh=mesh, in_specs=in_specs, out_specs=out_specs, check_vma=False)
```

```python
import jax
import jax.numpy as jnp
from jax import lax
from jax.sharding import PartitionSpec as P

keep_rate = 0.9


def gelu_tanh(values):
    return jax.nn.gelu(values, approximate=True)


def fold_slots(one_hot, slot_values):
    high_part = slot_values.astype(jnp.bfloat16)
    low_part = (slot_values - high_part.astype(jnp.float32)).astype(jnp.bfloat16)
    dims = (((0,), (0,)), ((), ()))
    return lax.dot_general(one_hot, high_part, dims, preferred_element_type=jnp.float32) + lax.dot_general(
        one_hot, low_part, dims, preferred_element_type=jnp.float32
    )


def body(tokens, cotangent, w_gate, w_up, w_down, slot_token, slot_weight, keep_mask):
    gate_mat = w_gate[0]
    up_mat = w_up[0]
    down_mat = w_down[0]
    model_width, local_ff = gate_mat.shape
    hidden_count = lax.axis_size("hidden")
    expert_count = lax.axis_size("expert")
    expert_total, per_source = slot_token.shape
    slot_count = expert_count * per_source
    group_tokens, local_width = tokens.shape
    slot_list = slot_token.reshape(-1)
    weight_column = slot_weight.reshape(-1, 1)
    inv_keep = 1.0 / keep_rate

    chosen = tokens[slot_list]
    scaled = (weight_column * cotangent[slot_list].astype(jnp.float32)).astype(jnp.bfloat16)
    slab = jnp.concatenate([chosen, scaled], axis=1).reshape(expert_total, per_source, 2 * local_width)
    recv = lax.all_to_all(slab, "expert", split_axis=0, concat_axis=0, tiled=True)
    slab_slots = recv.reshape(slot_count, 2 * local_width)
    gathered = lax.all_gather(slab_slots, "hidden", axis=0, tiled=False)
    part_inputs = gathered[:, :, :local_width]
    part_cot = gathered[:, :, local_width:]

    gate_rows = gate_mat.reshape(hidden_count, local_width, local_ff)
    up_rows = up_mat.reshape(hidden_count, local_width, local_ff)
    down_cols = down_mat.reshape(local_ff, hidden_count, local_width)
    fwd_dims = (((0, 2), (0, 1)), ((), ()))
    gate_pre = lax.dot_general(part_inputs, gate_rows, fwd_dims, preferred_element_type=jnp.float32)
    up_pre = lax.dot_general(part_inputs, up_rows, fwd_dims, preferred_element_type=jnp.float32)
    grad_hidden = lax.dot_general(
        part_cot, down_cols, (((0, 2), (1, 2)), ((), ())), preferred_element_type=jnp.float32
    )
    activated, pullback = jax.vjp(gelu_tanh, gate_pre)
    grad_pre = grad_hidden * keep_mask[0].astype(jnp.float32) * inv_keep
    grad_up = (grad_pre * activated).astype(jnp.bfloat16)
    grad_gate = pullback(grad_pre * up_pre)[0].astype(jnp.bfloat16)
    grad_gate, grad_up = lax.optimization_barrier((grad_gate, grad_up))

    back_dims = (((1,), (1,)), ((), ()))
    partial = lax.dot_general(
        grad_gate, gate_mat, back_dims, preferred_element_type=jnp.float32
    ) + lax.dot_general(grad_up, up_mat, back_dims, preferred_element_type=jnp.float32)
    blocks = partial.reshape(expert_count, per_source, hidden_count, local_width).transpose(0, 2, 1, 3)
    blocks = blocks.astype(jnp.bfloat16).reshape(expert_count * hidden_count, per_source, local_width)
    returned = lax.all_to_all(blocks, ("expert", "hidden"), split_axis=0, concat_axis=0, tiled=True)
    per_expert = returned.reshape(expert_total, hidden_count, per_source, local_width).astype(jnp.float32).sum(1)
    one_hot = (slot_list[:, None] == jnp.arange(group_tokens, dtype=jnp.int32)[None, :]).astype(jnp.bfloat16)
    token_sum = fold_slots(one_hot, per_expert.reshape(expert_total * per_source, local_width))
    return token_sum.astype(jnp.bfloat16)


def solution(mesh):
    in_specs = (
        P("expert", "hidden"),
        P("expert", "hidden"),
        P("expert", None, "hidden"),
        P("expert", None, "hidden"),
        P("expert", "hidden", None),
        P(None, "expert"),
        P(None, "expert"),
        P("expert", None, "hidden"),
    )
    out_specs = P("expert", "hidden")
    return jax.shard_map(body, mesh=mesh, in_specs=in_specs, out_specs=out_specs, check_vma=False)
```

```python
import jax
import jax.numpy as jnp
from jax import lax
from jax.sharding import Mesh
from jax.sharding import PartitionSpec as P

keep_rate = 0.9
CROSS = ("expert", "chip")
HIDDEN = ("chip", "core")


def gelu_tanh(values):
    return jax.nn.gelu(values, approximate=True)


def fold_slots(one_hot, slot_values):
    high_part = slot_values.astype(jnp.bfloat16)
    low_part = (slot_values - high_part.astype(jnp.float32)).astype(jnp.bfloat16)
    dims = (((0,), (0,)), ((), ()))
    return lax.dot_general(one_hot, high_part, dims, preferred_element_type=jnp.float32) + lax.dot_general(
        one_hot, low_part, dims, preferred_element_type=jnp.float32
    )


def order_by_core(own, other, axis):
    first = lax.axis_index("core") == 0
    low = jnp.where(first, own, other)
    high = jnp.where(first, other, own)
    return jnp.stack([low, high], axis=axis)


def swap_cores(values):
    return lax.ppermute(values, "core", [(0, 1), (1, 0)])


def body(tokens, cotangent, w_gate, w_up, w_down, slot_token, slot_weight, keep_mask):
    gate_mat = w_gate[0]
    up_mat = w_up[0]
    down_mat = w_down[0]
    model_width, local_ff = gate_mat.shape
    chip_count = lax.axis_size("chip")
    expert_count = lax.axis_size("expert")
    expert_total, per_source = slot_token.shape
    slot_count = expert_count * per_source
    group_tokens, local_width = tokens.shape
    slot_list = slot_token.reshape(-1)
    weight_column = slot_weight.reshape(-1, 1)
    inv_keep = 1.0 / keep_rate

    chosen = tokens[slot_list]
    scaled = (weight_column * cotangent[slot_list].astype(jnp.float32)).astype(jnp.bfloat16)
    slab = jnp.concatenate([chosen, scaled], axis=1).reshape(expert_total, 1, per_source, 2 * local_width)
    outgoing = jnp.broadcast_to(slab, (expert_total, chip_count, per_source, 2 * local_width))
    outgoing = outgoing.reshape(expert_total * chip_count, per_source, 2 * local_width)
    own = lax.all_to_all(outgoing, CROSS, split_axis=0, concat_axis=0, tiled=True)
    own = own.reshape(expert_count, chip_count, per_source, 2 * local_width)
    other = swap_cores(own)
    full = order_by_core(own, other, axis=2)
    part_inputs = full[..., :local_width]
    part_cot = full[..., local_width:]

    gate_rows = gate_mat.reshape(chip_count, 2, local_width, local_ff)
    up_rows = up_mat.reshape(chip_count, 2, local_width, local_ff)
    down_cols = down_mat.reshape(local_ff, chip_count, 2, local_width)
    fwd_dims = (((1, 2, 4), (0, 1, 2)), ((), ()))
    gate_pre = lax.dot_general(part_inputs, gate_rows, fwd_dims, preferred_element_type=jnp.float32)
    up_pre = lax.dot_general(part_inputs, up_rows, fwd_dims, preferred_element_type=jnp.float32)
    grad_hidden = lax.dot_general(
        part_cot, down_cols, (((1, 2, 4), (1, 2, 3)), ((), ())), preferred_element_type=jnp.float32
    )
    gate_pre = gate_pre.reshape(slot_count, local_ff)
    up_pre = up_pre.reshape(slot_count, local_ff)
    grad_hidden = grad_hidden.reshape(slot_count, local_ff)
    activated, pullback = jax.vjp(gelu_tanh, gate_pre)
    grad_pre = grad_hidden * keep_mask[0].astype(jnp.float32) * inv_keep
    grad_up = (grad_pre * activated).astype(jnp.bfloat16)
    grad_gate = pullback(grad_pre * up_pre)[0].astype(jnp.bfloat16)
    grad_gate, grad_up = lax.optimization_barrier((grad_gate, grad_up))

    back_dims = (((1,), (1,)), ((), ()))
    partial = lax.dot_general(
        grad_gate, gate_mat, back_dims, preferred_element_type=jnp.float32
    ) + lax.dot_general(grad_up, up_mat, back_dims, preferred_element_type=jnp.float32)
    partial = partial.reshape(expert_count, per_source, chip_count, 2, local_width)
    first = lax.axis_index("core") == 0
    keep_half = jnp.where(first, partial[:, :, :, 0], partial[:, :, :, 1])
    send_half = jnp.where(first, partial[:, :, :, 1], partial[:, :, :, 0]).astype(jnp.bfloat16)
    chip_sum = keep_half + swap_cores(send_half).astype(jnp.float32)
    blocks = chip_sum.astype(jnp.bfloat16).transpose(0, 2, 1, 3)
    blocks = blocks.reshape(expert_count * chip_count, per_source, local_width)
    returned = lax.all_to_all(blocks, CROSS, split_axis=0, concat_axis=0, tiled=True)
    per_expert = returned.reshape(expert_total, chip_count, per_source, local_width).astype(jnp.float32).sum(1)
    one_hot = (slot_list[:, None] == jnp.arange(group_tokens, dtype=jnp.int32)[None, :]).astype(jnp.bfloat16)
    token_sum = fold_slots(one_hot, per_expert.reshape(expert_total * per_source, local_width))
    return token_sum.astype(jnp.bfloat16)


def solution(mesh):
    expert_count, hidden_count = mesh.devices.shape
    split_mesh = Mesh(mesh.devices.reshape(expert_count, hidden_count // 2, 2), ("expert", "chip", "core"))
    in_specs = (
        P("expert", HIDDEN),
        P("expert", HIDDEN),
        P("expert", None, HIDDEN),
        P("expert", None, HIDDEN),
        P("expert", HIDDEN, None),
        P(None, "expert"),
        P(None, "expert"),
        P("expert", None, HIDDEN),
    )
    out_specs = P("expert", HIDDEN)
    return jax.shard_map(body, mesh=split_mesh, in_specs=in_specs, out_specs=out_specs, check_vma=False)
```

```python
import jax
import jax.numpy as jnp
from jax import lax
from jax.sharding import Mesh
from jax.sharding import PartitionSpec as P

keep_rate = 0.9
CROSS = ("expert", "chip")
HIDDEN = ("chip", "core")


def gelu_tanh(values):
    return jax.nn.gelu(values, approximate=True)


def fold_slots(one_hot, slot_values):
    high_part = slot_values.astype(jnp.bfloat16)
    low_part = (slot_values - high_part.astype(jnp.float32)).astype(jnp.bfloat16)
    dims = (((0,), (0,)), ((), ()))
    return lax.dot_general(one_hot, high_part, dims, preferred_element_type=jnp.float32) + lax.dot_general(
        one_hot, low_part, dims, preferred_element_type=jnp.float32
    )


def order_by_core(own, other, axis):
    first = lax.axis_index("core") == 0
    low = jnp.where(first, own, other)
    high = jnp.where(first, other, own)
    return jnp.stack([low, high], axis=axis)


def swap_cores(values):
    return lax.ppermute(values, "core", [(0, 1), (1, 0)])


def body(tokens, cotangent, w_gate, w_up, w_down, slot_token, slot_weight, keep_mask):
    gate_mat = w_gate[0]
    up_mat = w_up[0]
    down_mat = w_down[0]
    model_width, local_ff = gate_mat.shape
    chip_count = lax.axis_size("chip")
    expert_count = lax.axis_size("expert")
    expert_total, per_source = slot_token.shape
    slot_count = expert_count * per_source
    group_tokens, local_width = tokens.shape
    slot_list = slot_token.reshape(-1)
    weight_column = slot_weight.reshape(-1, 1)
    inv_keep = 1.0 / keep_rate

    chosen = tokens[slot_list]
    scaled = (weight_column * cotangent[slot_list].astype(jnp.float32)).astype(jnp.bfloat16)
    slab = jnp.concatenate([chosen, scaled], axis=1).reshape(expert_total, 1, per_source, 2 * local_width)
    outgoing = jnp.broadcast_to(slab, (expert_total, chip_count, per_source, 2 * local_width))
    outgoing = outgoing.reshape(expert_total * chip_count, per_source, 2 * local_width)
    own = lax.all_to_all(outgoing, CROSS, split_axis=0, concat_axis=0, tiled=True)
    own = own.reshape(expert_count, chip_count, per_source, 2 * local_width)
    other = swap_cores(own)
    full = order_by_core(own, other, axis=2)
    part_inputs = full[..., :local_width]
    cot_t = full[..., local_width:].transpose(1, 2, 4, 0, 3).reshape(model_width, slot_count)

    gate_rows = gate_mat.reshape(chip_count, 2, local_width, local_ff)
    up_rows = up_mat.reshape(chip_count, 2, local_width, local_ff)
    fwd_dims = (((1, 2, 4), (0, 1, 2)), ((), ()))
    gate_pre = lax.dot_general(part_inputs, gate_rows, fwd_dims, preferred_element_type=jnp.float32)
    up_pre = lax.dot_general(part_inputs, up_rows, fwd_dims, preferred_element_type=jnp.float32)
    hidden_t = jnp.dot(down_mat, cot_t, preferred_element_type=jnp.float32)
    gate_pre = gate_pre.reshape(slot_count, local_ff)
    up_pre = up_pre.reshape(slot_count, local_ff)
    grad_hidden = hidden_t.reshape(local_ff, slot_count).T
    activated, pullback = jax.vjp(gelu_tanh, gate_pre)
    grad_pre = grad_hidden * keep_mask[0].astype(jnp.float32) * inv_keep
    grad_up = (grad_pre * activated).astype(jnp.bfloat16)
    grad_gate = pullback(grad_pre * up_pre)[0].astype(jnp.bfloat16)
    grad_gate, grad_up = lax.optimization_barrier((grad_gate, grad_up))

    back_dims = (((1,), (1,)), ((), ()))
    partial = lax.dot_general(
        gate_mat, grad_gate, back_dims, preferred_element_type=jnp.float32
    ) + lax.dot_general(up_mat, grad_up, back_dims, preferred_element_type=jnp.float32)
    partial = partial.reshape(chip_count, 2, local_width, slot_count)
    first = lax.axis_index("core") == 0
    keep_half = jnp.where(first, partial[:, 0], partial[:, 1])
    send_half = jnp.where(first, partial[:, 1], partial[:, 0]).astype(jnp.bfloat16)
    chip_sum = keep_half + swap_cores(send_half).astype(jnp.float32)
    blocks = chip_sum.astype(jnp.bfloat16).reshape(chip_count, local_width, expert_count, per_source)
    blocks = blocks.transpose(2, 0, 1, 3).reshape(expert_count * chip_count, local_width, per_source)
    returned = lax.all_to_all(blocks, CROSS, split_axis=0, concat_axis=0, tiled=True)
    per_expert = returned.reshape(expert_total, chip_count, local_width, per_source).astype(jnp.float32).sum(1)
    per_expert = per_expert.transpose(0, 2, 1).reshape(expert_total * per_source, local_width)
    one_hot = (slot_list[:, None] == jnp.arange(group_tokens, dtype=jnp.int32)[None, :]).astype(jnp.bfloat16)
    token_sum = fold_slots(one_hot, per_expert)
    return token_sum.astype(jnp.bfloat16)


def solution(mesh):
    expert_count, hidden_count = mesh.devices.shape
    split_mesh = Mesh(mesh.devices.reshape(expert_count, hidden_count // 2, 2), ("expert", "chip", "core"))
    in_specs = (
        P("expert", HIDDEN),
        P("expert", HIDDEN),
        P("expert", None, HIDDEN),
        P("expert", None, HIDDEN),
        P("expert", HIDDEN, None),
        P(None, "expert"),
        P(None, "expert"),
        P("expert", None, HIDDEN),
    )
    out_specs = P("expert", HIDDEN)
    return jax.shard_map(body, mesh=split_mesh, in_specs=in_specs, out_specs=out_specs, check_vma=False)
```

```python
import math

import jax
import jax.numpy as jnp
from jax import lax
from jax.experimental import pallas as pl
from jax.experimental.pallas import tpu as pltpu
from jax.sharding import Mesh
from jax.sharding import PartitionSpec as P

keep_rate = 0.9
CROSS = ("expert", "chip")
HIDDEN = ("chip", "core")
GELU_C = math.sqrt(2.0 / math.pi)
GELU_A = 0.044715


def gelu_tanh(values):
    return jax.nn.gelu(values, approximate=True)


def expert_kernel(x_ref, dy_ref, wg_ref, wu_ref, wd_ref, mask_ref, out_ref):
    @pl.when(pl.program_id(0) == 0)
    def _():
        out_ref[...] = jnp.zeros_like(out_ref)

    x = x_ref[...]
    wg = wg_ref[...]
    wu = wu_ref[...]
    gate_pre = jnp.dot(x, wg, preferred_element_type=jnp.float32)
    up_pre = jnp.dot(x, wu, preferred_element_type=jnp.float32)
    nt = (((1,), (1,)), ((), ()))
    grad_hidden = lax.dot_general(dy_ref[...], wd_ref[...], nt, preferred_element_type=jnp.float32)
    grad_pre = grad_hidden * mask_ref[...].astype(jnp.float32) * (1.0 / keep_rate)
    inner = GELU_C * (gate_pre + GELU_A * gate_pre * gate_pre * gate_pre)
    t = jnp.tanh(inner)
    activated = 0.5 * gate_pre * (1.0 + t)
    slope = 0.5 * (1.0 + t) + 0.5 * gate_pre * (1.0 - t * t) * GELU_C * (1.0 + 3.0 * GELU_A * gate_pre * gate_pre)
    grad_up = (grad_pre * activated).astype(jnp.bfloat16)
    grad_gate = (grad_pre * up_pre * slope).astype(jnp.bfloat16)
    out_ref[...] += lax.dot_general(grad_gate, wg, nt, preferred_element_type=jnp.float32) + lax.dot_general(
        grad_up, wu, nt, preferred_element_type=jnp.float32
    )


def expert_grad(x, dy, wg, wu, wd, mask, tile=256):
    slots, width = x.shape
    ff = wg.shape[1]
    tile = min(tile, ff)
    return pl.pallas_call(
        expert_kernel,
        grid=(ff // tile,),
        in_specs=[
            pl.BlockSpec((slots, width), lambda f: (0, 0)),
            pl.BlockSpec((slots, width), lambda f: (0, 0)),
            pl.BlockSpec((width, tile), lambda f: (0, f)),
            pl.BlockSpec((width, tile), lambda f: (0, f)),
            pl.BlockSpec((tile, width), lambda f: (f, 0)),
            pl.BlockSpec((slots, tile), lambda f: (0, f)),
        ],
        out_specs=pl.BlockSpec((slots, width), lambda f: (0, 0)),
        out_shape=jax.ShapeDtypeStruct((slots, width), jnp.float32),
        compiler_params=pltpu.CompilerParams(dimension_semantics=("arbitrary",), vmem_limit_bytes=48 * 1024 * 1024),
    )(x, dy, wg, wu, wd, mask)


def fold_slots(one_hot, slot_values):
    high_part = slot_values.astype(jnp.bfloat16)
    low_part = (slot_values - high_part.astype(jnp.float32)).astype(jnp.bfloat16)
    dims = (((0,), (0,)), ((), ()))
    return lax.dot_general(one_hot, high_part, dims, preferred_element_type=jnp.float32) + lax.dot_general(
        one_hot, low_part, dims, preferred_element_type=jnp.float32
    )


def order_by_core(own, other, axis):
    first = lax.axis_index("core") == 0
    low = jnp.where(first, own, other)
    high = jnp.where(first, other, own)
    return jnp.stack([low, high], axis=axis)


def swap_cores(values):
    return lax.ppermute(values, "core", [(0, 1), (1, 0)])


def body(tokens, cotangent, w_gate, w_up, w_down, slot_token, slot_weight, keep_mask):
    gate_mat = w_gate[0]
    up_mat = w_up[0]
    down_mat = w_down[0]
    model_width, local_ff = gate_mat.shape
    chip_count = lax.axis_size("chip")
    expert_count = lax.axis_size("expert")
    expert_total, per_source = slot_token.shape
    slot_count = expert_count * per_source
    group_tokens, local_width = tokens.shape
    slot_list = slot_token.reshape(-1)
    weight_column = slot_weight.reshape(-1, 1)
    inv_keep = 1.0 / keep_rate

    chosen = tokens[slot_list]
    scaled = (weight_column * cotangent[slot_list].astype(jnp.float32)).astype(jnp.bfloat16)
    slab = jnp.concatenate([chosen, scaled], axis=1).reshape(expert_total, 1, per_source, 2 * local_width)
    outgoing = jnp.broadcast_to(slab, (expert_total, chip_count, per_source, 2 * local_width))
    outgoing = outgoing.reshape(expert_total * chip_count, per_source, 2 * local_width)
    own = lax.all_to_all(outgoing, CROSS, split_axis=0, concat_axis=0, tiled=True)
    own = own.reshape(expert_count, chip_count, per_source, 2 * local_width)
    other = swap_cores(own)
    full = order_by_core(own, other, axis=2)
    part_inputs = full[..., :local_width].transpose(0, 3, 1, 2, 4).reshape(slot_count, model_width)
    part_cot = full[..., local_width:].transpose(0, 3, 1, 2, 4).reshape(slot_count, model_width)
    partial = expert_grad(part_inputs, part_cot, gate_mat, up_mat, down_mat, keep_mask[0])
    partial = partial.reshape(expert_count, per_source, chip_count, 2, local_width)
    first = lax.axis_index("core") == 0
    keep_half = jnp.where(first, partial[:, :, :, 0], partial[:, :, :, 1])
    send_half = jnp.where(first, partial[:, :, :, 1], partial[:, :, :, 0]).astype(jnp.bfloat16)
    chip_sum = keep_half + swap_cores(send_half).astype(jnp.float32)
    blocks = chip_sum.astype(jnp.bfloat16).transpose(0, 2, 1, 3)
    blocks = blocks.reshape(expert_count * chip_count, per_source, local_width)
    returned = lax.all_to_all(blocks, CROSS, split_axis=0, concat_axis=0, tiled=True)
    per_expert = returned.reshape(expert_total, chip_count, per_source, local_width).astype(jnp.float32).sum(1)
    one_hot = (slot_list[:, None] == jnp.arange(group_tokens, dtype=jnp.int32)[None, :]).astype(jnp.bfloat16)
    token_sum = fold_slots(one_hot, per_expert.reshape(expert_total * per_source, local_width))
    return token_sum.astype(jnp.bfloat16)


def solution(mesh):
    expert_count, hidden_count = mesh.devices.shape
    split_mesh = Mesh(mesh.devices.reshape(expert_count, hidden_count // 2, 2), ("expert", "chip", "core"))
    in_specs = (
        P("expert", HIDDEN),
        P("expert", HIDDEN),
        P("expert", None, HIDDEN),
        P("expert", None, HIDDEN),
        P("expert", HIDDEN, None),
        P(None, "expert"),
        P(None, "expert"),
        P("expert", None, HIDDEN),
    )
    out_specs = P("expert", HIDDEN)
    return jax.shard_map(body, mesh=split_mesh, in_specs=in_specs, out_specs=out_specs, check_vma=False)
```

```python
import math

import jax
import jax.numpy as jnp
from jax import lax
from jax.experimental import pallas as pl
from jax.experimental.pallas import tpu as pltpu
from jax.sharding import Mesh
from jax.sharding import PartitionSpec as P

keep_rate = 0.9
CROSS = ("expert", "chip")
HIDDEN = ("chip", "core")
GELU_C = math.sqrt(2.0 / math.pi)
GELU_A = 0.044715


def gelu_tanh(values):
    return jax.nn.gelu(values, approximate=True)


def expert_kernel(x_ref, dyt_ref, wg_ref, wu_ref, wd_ref, mask_ref, out_ref):
    @pl.when(pl.program_id(0) == 0)
    def _():
        out_ref[...] = jnp.zeros_like(out_ref)

    x = x_ref[...]
    wg = wg_ref[...]
    wu = wu_ref[...]
    gate_pre = jnp.dot(x, wg, preferred_element_type=jnp.float32)
    up_pre = jnp.dot(x, wu, preferred_element_type=jnp.float32)
    grad_hidden = jnp.dot(wd_ref[...], dyt_ref[...], preferred_element_type=jnp.float32).T
    grad_pre = grad_hidden * mask_ref[...].astype(jnp.float32) * (1.0 / keep_rate)
    inner = GELU_C * (gate_pre + GELU_A * gate_pre * gate_pre * gate_pre)
    t = jnp.tanh(inner)
    activated = 0.5 * gate_pre * (1.0 + t)
    slope = 0.5 * (1.0 + t) + 0.5 * gate_pre * (1.0 - t * t) * GELU_C * (1.0 + 3.0 * GELU_A * gate_pre * gate_pre)
    grad_up = (grad_pre * activated).astype(jnp.bfloat16)
    grad_gate = (grad_pre * up_pre * slope).astype(jnp.bfloat16)
    nt = (((1,), (1,)), ((), ()))
    out_ref[...] += lax.dot_general(wg, grad_gate, nt, preferred_element_type=jnp.float32) + lax.dot_general(
        wu, grad_up, nt, preferred_element_type=jnp.float32
    )


def expert_grad(x, dyt, wg, wu, wd, mask, tile=256):
    slots, width = x.shape
    ff = wg.shape[1]
    tile = min(tile, ff)
    return pl.pallas_call(
        expert_kernel,
        grid=(ff // tile,),
        in_specs=[
            pl.BlockSpec((slots, width), lambda f: (0, 0)),
            pl.BlockSpec((width, slots), lambda f: (0, 0)),
            pl.BlockSpec((width, tile), lambda f: (0, f)),
            pl.BlockSpec((width, tile), lambda f: (0, f)),
            pl.BlockSpec((tile, width), lambda f: (f, 0)),
            pl.BlockSpec((slots, tile), lambda f: (0, f)),
        ],
        out_specs=pl.BlockSpec((width, slots), lambda f: (0, 0)),
        out_shape=jax.ShapeDtypeStruct((width, slots), jnp.float32),
        compiler_params=pltpu.CompilerParams(dimension_semantics=("arbitrary",), vmem_limit_bytes=48 * 1024 * 1024),
    )(x, dyt, wg, wu, wd, mask)


def fold_slots(one_hot, slot_values):
    high_part = slot_values.astype(jnp.bfloat16)
    low_part = (slot_values - high_part.astype(jnp.float32)).astype(jnp.bfloat16)
    dims = (((0, 1), (0, 2)), ((), ()))
    return lax.dot_general(one_hot, high_part, dims, preferred_element_type=jnp.float32) + lax.dot_general(
        one_hot, low_part, dims, preferred_element_type=jnp.float32
    )


def order_by_core(own, other, axis):
    first = lax.axis_index("core") == 0
    low = jnp.where(first, own, other)
    high = jnp.where(first, other, own)
    return jnp.stack([low, high], axis=axis)


def swap_cores(values):
    return lax.ppermute(values, "core", [(0, 1), (1, 0)])


def body(tokens, cotangent, w_gate, w_up, w_down, slot_token, slot_weight, keep_mask):
    gate_mat = w_gate[0]
    up_mat = w_up[0]
    down_mat = w_down[0]
    model_width, local_ff = gate_mat.shape
    chip_count = lax.axis_size("chip")
    expert_count = lax.axis_size("expert")
    expert_total, per_source = slot_token.shape
    slot_count = expert_count * per_source
    group_tokens, local_width = tokens.shape
    slot_list = slot_token.reshape(-1)
    weight_column = slot_weight.reshape(-1, 1)
    inv_keep = 1.0 / keep_rate

    chosen = tokens[slot_list]
    scaled = (weight_column * cotangent[slot_list].astype(jnp.float32)).astype(jnp.bfloat16)
    slab = jnp.concatenate([chosen, scaled], axis=1).reshape(expert_total, 1, per_source, 2 * local_width)
    outgoing = jnp.broadcast_to(slab, (expert_total, chip_count, per_source, 2 * local_width))
    outgoing = outgoing.reshape(expert_total * chip_count, per_source, 2 * local_width)
    own = lax.all_to_all(outgoing, CROSS, split_axis=0, concat_axis=0, tiled=True)
    own = own.reshape(expert_count, chip_count, per_source, 2 * local_width)
    other = swap_cores(own)
    full = order_by_core(own, other, axis=2)
    part_inputs = full[..., :local_width].transpose(0, 3, 1, 2, 4).reshape(slot_count, model_width)
    cot_t = full[..., local_width:].transpose(1, 2, 4, 0, 3).reshape(model_width, slot_count)
    partial = expert_grad(part_inputs, cot_t, gate_mat, up_mat, down_mat, keep_mask[0])
    partial = partial.reshape(chip_count, 2, local_width, slot_count)
    first = lax.axis_index("core") == 0
    keep_half = jnp.where(first, partial[:, 0], partial[:, 1])
    send_half = jnp.where(first, partial[:, 1], partial[:, 0]).astype(jnp.bfloat16)
    chip_sum = keep_half + swap_cores(send_half).astype(jnp.float32)
    blocks = chip_sum.astype(jnp.bfloat16).reshape(chip_count, local_width, expert_count, per_source)
    blocks = blocks.transpose(2, 0, 1, 3).reshape(expert_count * chip_count, local_width, per_source)
    returned = lax.all_to_all(blocks, CROSS, split_axis=0, concat_axis=0, tiled=True)
    per_expert = returned.reshape(expert_total, chip_count, local_width, per_source).astype(jnp.float32).sum(1)
    one_hot = (slot_list[:, None] == jnp.arange(group_tokens, dtype=jnp.int32)[None, :]).astype(jnp.bfloat16)
    one_hot = one_hot.reshape(expert_total, per_source, group_tokens)
    token_sum = fold_slots(one_hot, per_expert)
    return token_sum.astype(jnp.bfloat16)


def solution(mesh):
    expert_count, hidden_count = mesh.devices.shape
    split_mesh = Mesh(mesh.devices.reshape(expert_count, hidden_count // 2, 2), ("expert", "chip", "core"))
    in_specs = (
        P("expert", HIDDEN),
        P("expert", HIDDEN),
        P("expert", None, HIDDEN),
        P("expert", None, HIDDEN),
        P("expert", HIDDEN, None),
        P(None, "expert"),
        P(None, "expert"),
        P("expert", None, HIDDEN),
    )
    out_specs = P("expert", HIDDEN)
    return jax.shard_map(body, mesh=split_mesh, in_specs=in_specs, out_specs=out_specs, check_vma=False)
```

```python
import jax
import jax.numpy as jnp
from jax import lax
from jax.sharding import Mesh
from jax.sharding import PartitionSpec as P

keep_rate = 0.9
CROSS = ("expert", "chip")
HIDDEN = ("chip", "core")


def gelu_tanh(values):
    return jax.nn.gelu(values, approximate=True)


def fold_slots(one_hot, slot_values):
    high_part = slot_values.astype(jnp.bfloat16)
    low_part = (slot_values - high_part.astype(jnp.float32)).astype(jnp.bfloat16)
    dims = (((0,), (0,)), ((), ()))
    return lax.dot_general(one_hot, high_part, dims, preferred_element_type=jnp.float32) + lax.dot_general(
        one_hot, low_part, dims, preferred_element_type=jnp.float32
    )


def order_by_core(own, other, axis):
    first = lax.axis_index("core") == 0
    low = jnp.where(first, own, other)
    high = jnp.where(first, other, own)
    return jnp.stack([low, high], axis=axis)


def swap_cores(values):
    return lax.ppermute(values, "core", [(0, 1), (1, 0)])


def body(tokens, cotangent, w_gate, w_up, w_down, slot_token, slot_weight, keep_mask):
    gate_mat = w_gate[0]
    up_mat = w_up[0]
    down_mat = w_down[0]
    model_width, local_ff = gate_mat.shape
    chip_count = lax.axis_size("chip")
    expert_count = lax.axis_size("expert")
    expert_total, per_source = slot_token.shape
    slot_count = expert_count * per_source
    group_tokens, local_width = tokens.shape
    slot_list = slot_token.reshape(-1)
    weight_column = slot_weight.reshape(-1, 1)
    inv_keep = 1.0 / keep_rate

    chosen = tokens[slot_list]
    scaled = (weight_column * cotangent[slot_list].astype(jnp.float32)).astype(jnp.bfloat16)
    slab = jnp.concatenate([chosen, scaled], axis=1).reshape(expert_total, 1, per_source, 2 * local_width)
    outgoing = jnp.broadcast_to(slab, (expert_total, chip_count, per_source, 2 * local_width))
    outgoing = outgoing.reshape(expert_total * chip_count, per_source, 2 * local_width)
    own = lax.all_to_all(outgoing, CROSS, split_axis=0, concat_axis=0, tiled=True)
    own = own.reshape(expert_count, chip_count, per_source, 2 * local_width)
    other = swap_cores(own)
    full = order_by_core(own, other, axis=2)
    part_inputs = full[..., :local_width]
    cot_t = full[..., local_width:].transpose(1, 2, 4, 0, 3).reshape(model_width, slot_count)

    gate_rows = gate_mat.reshape(chip_count, 2, local_width, local_ff)
    up_rows = up_mat.reshape(chip_count, 2, local_width, local_ff)
    fwd_dims = (((1, 2, 4), (0, 1, 2)), ((), ()))
    gate_pre = lax.dot_general(part_inputs, gate_rows, fwd_dims, preferred_element_type=jnp.float32)
    up_pre = lax.dot_general(part_inputs, up_rows, fwd_dims, preferred_element_type=jnp.float32)
    hidden_t = jnp.dot(down_mat, cot_t, preferred_element_type=jnp.float32)
    gate_pre = gate_pre.reshape(slot_count, local_ff)
    up_pre = up_pre.reshape(slot_count, local_ff)
    grad_hidden = hidden_t.T
    activated, pullback = jax.vjp(gelu_tanh, gate_pre)
    grad_pre = grad_hidden * keep_mask[0].astype(jnp.float32) * inv_keep
    grad_up = (grad_pre * activated).astype(jnp.bfloat16)
    grad_gate = pullback(grad_pre * up_pre)[0].astype(jnp.bfloat16)
    grad_gate, grad_up = lax.optimization_barrier((grad_gate, grad_up))

    back_dims = (((1,), (1,)), ((), ()))
    partial = lax.dot_general(
        grad_gate, gate_mat, back_dims, preferred_element_type=jnp.float32
    ) + lax.dot_general(grad_up, up_mat, back_dims, preferred_element_type=jnp.float32)
    partial = partial.reshape(expert_count, per_source, chip_count, 2, local_width)
    first = lax.axis_index("core") == 0
    keep_half = jnp.where(first, partial[:, :, :, 0], partial[:, :, :, 1])
    send_half = jnp.where(first, partial[:, :, :, 1], partial[:, :, :, 0]).astype(jnp.bfloat16)
    chip_sum = keep_half + swap_cores(send_half).astype(jnp.float32)
    blocks = chip_sum.astype(jnp.bfloat16).transpose(0, 2, 1, 3)
    blocks = blocks.reshape(expert_count * chip_count, per_source, local_width)
    returned = lax.all_to_all(blocks, CROSS, split_axis=0, concat_axis=0, tiled=True)
    per_expert = returned.reshape(expert_total, chip_count, per_source, local_width).astype(jnp.float32).sum(1)
    one_hot = (slot_list[:, None] == jnp.arange(group_tokens, dtype=jnp.int32)[None, :]).astype(jnp.bfloat16)
    token_sum = fold_slots(one_hot, per_expert.reshape(expert_total * per_source, local_width))
    return token_sum.astype(jnp.bfloat16)


def solution(mesh):
    expert_count, hidden_count = mesh.devices.shape
    split_mesh = Mesh(mesh.devices.reshape(expert_count, hidden_count // 2, 2), ("expert", "chip", "core"))
    in_specs = (
        P("expert", HIDDEN),
        P("expert", HIDDEN),
        P("expert", None, HIDDEN),
        P("expert", None, HIDDEN),
        P("expert", HIDDEN, None),
        P(None, "expert"),
        P(None, "expert"),
        P("expert", None, HIDDEN),
    )
    out_specs = P("expert", HIDDEN)
    return jax.shard_map(body, mesh=split_mesh, in_specs=in_specs, out_specs=out_specs, check_vma=False)
```

```python
import jax
import jax.numpy as jnp
from jax import lax
from jax.sharding import Mesh
from jax.sharding import PartitionSpec as P

keep_rate = 0.9
CROSS = ("expert", "chip")
HIDDEN = ("chip", "core")


def gelu_tanh(values):
    return jax.nn.gelu(values, approximate=True)


def fold_slots(one_hot, slot_values):
    high_part = slot_values.astype(jnp.bfloat16)
    low_part = (slot_values - high_part.astype(jnp.float32)).astype(jnp.bfloat16)
    dims = (((0,), (0,)), ((), ()))
    return lax.dot_general(one_hot, high_part, dims, preferred_element_type=jnp.float32) + lax.dot_general(
        one_hot, low_part, dims, preferred_element_type=jnp.float32
    )


def order_by_core(own, other, axis):
    first = lax.axis_index("core") == 0
    low = jnp.where(first, own, other)
    high = jnp.where(first, other, own)
    return jnp.stack([low, high], axis=axis)


def swap_cores(values):
    return lax.ppermute(values, "core", [(0, 1), (1, 0)])


def body(tokens, cotangent, w_gate, w_up, w_down, slot_token, slot_weight, keep_mask):
    gate_mat = w_gate[0]
    up_mat = w_up[0]
    down_mat = w_down[0]
    model_width, local_ff = gate_mat.shape
    chip_count = lax.axis_size("chip")
    expert_count = lax.axis_size("expert")
    expert_total, per_source = slot_token.shape
    slot_count = expert_count * per_source
    group_tokens, local_width = tokens.shape
    slot_list = slot_token.reshape(-1)
    weight_column = slot_weight.reshape(-1, 1)
    inv_keep = 1.0 / keep_rate

    chosen = tokens[slot_list]
    scaled = (weight_column * cotangent[slot_list].astype(jnp.float32)).astype(jnp.bfloat16)
    slab = jnp.concatenate([chosen, scaled], axis=1).reshape(expert_total, 1, per_source, 2 * local_width)
    outgoing = jnp.broadcast_to(slab, (expert_total, chip_count, per_source, 2 * local_width))
    outgoing = outgoing.reshape(expert_total * chip_count, per_source, 2 * local_width)
    own = lax.all_to_all(outgoing, CROSS, split_axis=0, concat_axis=0, tiled=True)
    own = own.reshape(expert_count, chip_count, per_source, 2 * local_width)
    other = swap_cores(own)
    full = order_by_core(own, other, axis=2)
    part_inputs = full[..., :local_width]
    part_cot = full[..., local_width:]

    gate_rows = gate_mat.reshape(chip_count, 2, local_width, local_ff)
    up_rows = up_mat.reshape(chip_count, 2, local_width, local_ff)
    down_cols = down_mat.reshape(local_ff, chip_count, 2, local_width)
    fwd_dims = (((1, 2, 4), (0, 1, 2)), ((), ()))
    gate_pre = lax.dot_general(part_inputs, gate_rows, fwd_dims, preferred_element_type=jnp.float32)
    up_pre = lax.dot_general(part_inputs, up_rows, fwd_dims, preferred_element_type=jnp.float32)
    grad_hidden = lax.dot_general(
        part_cot, down_cols, (((1, 2, 4), (1, 2, 3)), ((), ())), preferred_element_type=jnp.float32
    )
    gate_pre = gate_pre.reshape(slot_count, local_ff)
    up_pre = up_pre.reshape(slot_count, local_ff)
    grad_hidden = grad_hidden.reshape(slot_count, local_ff)
    activated, pullback = jax.vjp(gelu_tanh, gate_pre)
    grad_pre = grad_hidden * keep_mask[0].astype(jnp.float32) * inv_keep
    grad_up = (grad_pre * activated).astype(jnp.bfloat16)
    grad_gate = pullback(grad_pre * up_pre)[0].astype(jnp.bfloat16)
    grad_gate, grad_up = lax.optimization_barrier((grad_gate, grad_up))

    back_dims = (((1,), (1,)), ((), ()))
    partial = lax.dot_general(
        grad_gate, gate_mat, back_dims, preferred_element_type=jnp.float32
    ) + lax.dot_general(grad_up, up_mat, back_dims, preferred_element_type=jnp.float32)
    partial = partial.astype(jnp.bfloat16).reshape(expert_count, per_source, chip_count, 2, local_width)
    first = lax.axis_index("core") == 0
    keep_half = jnp.where(first, partial[:, :, :, 0], partial[:, :, :, 1])
    send_half = jnp.where(first, partial[:, :, :, 1], partial[:, :, :, 0])
    chip_sum = keep_half.astype(jnp.float32) + swap_cores(send_half).astype(jnp.float32)
    blocks = chip_sum.astype(jnp.bfloat16).transpose(0, 2, 1, 3)
    blocks = blocks.reshape(expert_count * chip_count, per_source, local_width)
    returned = lax.all_to_all(blocks, CROSS, split_axis=0, concat_axis=0, tiled=True)
    per_expert = returned.reshape(expert_total, chip_count, per_source, local_width).astype(jnp.float32).sum(1)
    one_hot = (slot_list[:, None] == jnp.arange(group_tokens, dtype=jnp.int32)[None, :]).astype(jnp.bfloat16)
    token_sum = fold_slots(one_hot, per_expert.reshape(expert_total * per_source, local_width))
    return token_sum.astype(jnp.bfloat16)


def solution(mesh):
    expert_count, hidden_count = mesh.devices.shape
    split_mesh = Mesh(mesh.devices.reshape(expert_count, hidden_count // 2, 2), ("expert", "chip", "core"))
    in_specs = (
        P("expert", HIDDEN),
        P("expert", HIDDEN),
        P("expert", None, HIDDEN),
        P("expert", None, HIDDEN),
        P("expert", HIDDEN, None),
        P(None, "expert"),
        P(None, "expert"),
        P("expert", None, HIDDEN),
    )
    out_specs = P("expert", HIDDEN)
    return jax.shard_map(body, mesh=split_mesh, in_specs=in_specs, out_specs=out_specs, check_vma=False)
```

```python
import jax
import jax.numpy as jnp
from jax import lax
from jax.experimental import pallas as pl
from jax.experimental.pallas import tpu as pltpu
from jax.sharding import Mesh
from jax.sharding import PartitionSpec as P

keep_rate = 0.9
CROSS = ("expert", "chip")
HIDDEN = ("chip", "core")


def gelu_tanh(values):
    return jax.nn.gelu(values, approximate=True)


def hidden_kernel(wd_ref, dyt_ref, out_ref):
    out_ref[...] = jnp.dot(wd_ref[...], dyt_ref[...], preferred_element_type=jnp.float32).T


def hidden_grad(wd, dyt, tile=256):
    ff, width = wd.shape
    slots = dyt.shape[1]
    tile = min(tile, ff)
    return pl.pallas_call(
        hidden_kernel,
        grid=(ff // tile,),
        in_specs=[
            pl.BlockSpec((tile, width), lambda f: (f, 0)),
            pl.BlockSpec((width, slots), lambda f: (0, 0)),
        ],
        out_specs=pl.BlockSpec((slots, tile), lambda f: (0, f)),
        out_shape=jax.ShapeDtypeStruct((slots, ff), jnp.float32),
        compiler_params=pltpu.CompilerParams(dimension_semantics=("arbitrary",)),
    )(wd, dyt)


def fold_slots(one_hot, slot_values):
    high_part = slot_values.astype(jnp.bfloat16)
    low_part = (slot_values - high_part.astype(jnp.float32)).astype(jnp.bfloat16)
    dims = (((0,), (0,)), ((), ()))
    return lax.dot_general(one_hot, high_part, dims, preferred_element_type=jnp.float32) + lax.dot_general(
        one_hot, low_part, dims, preferred_element_type=jnp.float32
    )


def order_by_core(own, other, axis):
    first = lax.axis_index("core") == 0
    low = jnp.where(first, own, other)
    high = jnp.where(first, other, own)
    return jnp.stack([low, high], axis=axis)


def swap_cores(values):
    return lax.ppermute(values, "core", [(0, 1), (1, 0)])


def body(tokens, cotangent, w_gate, w_up, w_down, slot_token, slot_weight, keep_mask):
    gate_mat = w_gate[0]
    up_mat = w_up[0]
    down_mat = w_down[0]
    model_width, local_ff = gate_mat.shape
    chip_count = lax.axis_size("chip")
    expert_count = lax.axis_size("expert")
    expert_total, per_source = slot_token.shape
    slot_count = expert_count * per_source
    group_tokens, local_width = tokens.shape
    slot_list = slot_token.reshape(-1)
    weight_column = slot_weight.reshape(-1, 1)
    inv_keep = 1.0 / keep_rate

    chosen = tokens[slot_list]
    scaled = (weight_column * cotangent[slot_list].astype(jnp.float32)).astype(jnp.bfloat16)
    slab = jnp.concatenate([chosen, scaled], axis=1).reshape(expert_total, 1, per_source, 2 * local_width)
    outgoing = jnp.broadcast_to(slab, (expert_total, chip_count, per_source, 2 * local_width))
    outgoing = outgoing.reshape(expert_total * chip_count, per_source, 2 * local_width)
    own = lax.all_to_all(outgoing, CROSS, split_axis=0, concat_axis=0, tiled=True)
    own = own.reshape(expert_count, chip_count, per_source, 2 * local_width)
    other = swap_cores(own)
    full = order_by_core(own, other, axis=2)
    part_inputs = full[..., :local_width]
    cot_t = full[..., local_width:].transpose(1, 2, 4, 0, 3).reshape(model_width, slot_count)

    gate_rows = gate_mat.reshape(chip_count, 2, local_width, local_ff)
    up_rows = up_mat.reshape(chip_count, 2, local_width, local_ff)
    fwd_dims = (((1, 2, 4), (0, 1, 2)), ((), ()))
    gate_pre = lax.dot_general(part_inputs, gate_rows, fwd_dims, preferred_element_type=jnp.float32)
    up_pre = lax.dot_general(part_inputs, up_rows, fwd_dims, preferred_element_type=jnp.float32)
    grad_hidden = hidden_grad(down_mat, cot_t)
    gate_pre = gate_pre.reshape(slot_count, local_ff)
    up_pre = up_pre.reshape(slot_count, local_ff)
    activated, pullback = jax.vjp(gelu_tanh, gate_pre)
    grad_pre = grad_hidden * keep_mask[0].astype(jnp.float32) * inv_keep
    grad_up = (grad_pre * activated).astype(jnp.bfloat16)
    grad_gate = pullback(grad_pre * up_pre)[0].astype(jnp.bfloat16)
    grad_gate, grad_up = lax.optimization_barrier((grad_gate, grad_up))

    back_dims = (((1,), (1,)), ((), ()))
    partial = lax.dot_general(
        grad_gate, gate_mat, back_dims, preferred_element_type=jnp.float32
    ) + lax.dot_general(grad_up, up_mat, back_dims, preferred_element_type=jnp.float32)
    partial = partial.astype(jnp.bfloat16).reshape(expert_count, per_source, chip_count, 2, local_width)
    first = lax.axis_index("core") == 0
    keep_half = jnp.where(first, partial[:, :, :, 0], partial[:, :, :, 1])
    send_half = jnp.where(first, partial[:, :, :, 1], partial[:, :, :, 0])
    chip_sum = keep_half.astype(jnp.float32) + swap_cores(send_half).astype(jnp.float32)
    blocks = chip_sum.astype(jnp.bfloat16).transpose(0, 2, 1, 3)
    blocks = blocks.reshape(expert_count * chip_count, per_source, local_width)
    returned = lax.all_to_all(blocks, CROSS, split_axis=0, concat_axis=0, tiled=True)
    per_expert = returned.reshape(expert_total, chip_count, per_source, local_width).astype(jnp.float32).sum(1)
    one_hot = (slot_list[:, None] == jnp.arange(group_tokens, dtype=jnp.int32)[None, :]).astype(jnp.bfloat16)
    token_sum = fold_slots(one_hot, per_expert.reshape(expert_total * per_source, local_width))
    return token_sum.astype(jnp.bfloat16)


def solution(mesh):
    expert_count, hidden_count = mesh.devices.shape
    split_mesh = Mesh(mesh.devices.reshape(expert_count, hidden_count // 2, 2), ("expert", "chip", "core"))
    in_specs = (
        P("expert", HIDDEN),
        P("expert", HIDDEN),
        P("expert", None, HIDDEN),
        P("expert", None, HIDDEN),
        P("expert", HIDDEN, None),
        P(None, "expert"),
        P(None, "expert"),
        P("expert", None, HIDDEN),
    )
    out_specs = P("expert", HIDDEN)
    return jax.shard_map(body, mesh=split_mesh, in_specs=in_specs, out_specs=out_specs, check_vma=False)
```

```python
import jax
import jax.numpy as jnp
from jax import lax
from jax.sharding import Mesh
from jax.sharding import PartitionSpec as P

keep_rate = 0.9
CROSS = ("expert", "chip")
HIDDEN = ("chip", "core")


def gelu_tanh(values):
    return jax.nn.gelu(values, approximate=True)


def fold_slots(one_hot, slot_values):
    high_part = slot_values.astype(jnp.bfloat16)
    low_part = (slot_values - high_part.astype(jnp.float32)).astype(jnp.bfloat16)
    dims = (((0,), (0,)), ((), ()))
    return lax.dot_general(one_hot, high_part, dims, preferred_element_type=jnp.float32) + lax.dot_general(
        one_hot, low_part, dims, preferred_element_type=jnp.float32
    )


def order_by_core(own, other, axis):
    first = lax.axis_index("core") == 0
    low = jnp.where(first, own, other)
    high = jnp.where(first, other, own)
    return jnp.stack([low, high], axis=axis)


def swap_cores(values):
    return lax.ppermute(values, "core", [(0, 1), (1, 0)])


def body(tokens, cotangent, w_gate, w_up, w_down, slot_token, slot_weight, keep_mask):
    gate_mat = w_gate[0]
    up_mat = w_up[0]
    down_mat = w_down[0]
    model_width, local_ff = gate_mat.shape
    chip_count = lax.axis_size("chip")
    expert_count = lax.axis_size("expert")
    expert_total, per_source = slot_token.shape
    slot_count = expert_count * per_source
    group_tokens, local_width = tokens.shape
    slot_list = slot_token.reshape(-1)
    weight_column = slot_weight.reshape(-1, 1)
    inv_keep = 1.0 / keep_rate

    chosen = tokens[slot_list]
    scaled = (weight_column * cotangent[slot_list].astype(jnp.float32)).astype(jnp.bfloat16)
    slab = jnp.concatenate([chosen, scaled], axis=1).reshape(expert_total, 1, per_source, 2 * local_width)
    outgoing = jnp.broadcast_to(slab, (expert_total, chip_count, per_source, 2 * local_width))
    outgoing = outgoing.reshape(expert_total * chip_count, per_source, 2 * local_width)
    own = lax.all_to_all(outgoing, CROSS, split_axis=0, concat_axis=0, tiled=True)
    own = own.reshape(expert_count, chip_count, per_source, 2 * local_width)
    other = swap_cores(own)
    full = order_by_core(own, other, axis=2)
    part_inputs = full[..., :local_width]
    part_cot = full[..., local_width:].transpose(0, 3, 1, 2, 4).reshape(slot_count, model_width)

    gate_rows = gate_mat.reshape(chip_count, 2, local_width, local_ff)
    up_rows = up_mat.reshape(chip_count, 2, local_width, local_ff)
    fwd_dims = (((1, 2, 4), (0, 1, 2)), ((), ()))
    gate_pre = lax.dot_general(part_inputs, gate_rows, fwd_dims, preferred_element_type=jnp.float32)
    up_pre = lax.dot_general(part_inputs, up_rows, fwd_dims, preferred_element_type=jnp.float32)
    grad_hidden = lax.dot_general(
        part_cot, down_mat, (((1,), (1,)), ((), ())), preferred_element_type=jnp.float32
    )
    gate_pre = gate_pre.reshape(slot_count, local_ff)
    up_pre = up_pre.reshape(slot_count, local_ff)
    activated, pullback = jax.vjp(gelu_tanh, gate_pre)
    grad_pre = grad_hidden * keep_mask[0].astype(jnp.float32) * inv_keep
    grad_up = (grad_pre * activated).astype(jnp.bfloat16)
    grad_gate = pullback(grad_pre * up_pre)[0].astype(jnp.bfloat16)
    grad_gate, grad_up = lax.optimization_barrier((grad_gate, grad_up))

    back_dims = (((1,), (1,)), ((), ()))
    partial = lax.dot_general(
        grad_gate, gate_mat, back_dims, preferred_element_type=jnp.float32
    ) + lax.dot_general(grad_up, up_mat, back_dims, preferred_element_type=jnp.float32)
    partial = partial.astype(jnp.bfloat16).reshape(expert_count, per_source, chip_count, 2, local_width)
    first = lax.axis_index("core") == 0
    keep_half = jnp.where(first, partial[:, :, :, 0], partial[:, :, :, 1])
    send_half = jnp.where(first, partial[:, :, :, 1], partial[:, :, :, 0])
    chip_sum = keep_half.astype(jnp.float32) + swap_cores(send_half).astype(jnp.float32)
    blocks = chip_sum.astype(jnp.bfloat16).transpose(0, 2, 1, 3)
    blocks = blocks.reshape(expert_count * chip_count, per_source, local_width)
    returned = lax.all_to_all(blocks, CROSS, split_axis=0, concat_axis=0, tiled=True)
    per_expert = returned.reshape(expert_total, chip_count, per_source, local_width).astype(jnp.float32).sum(1)
    one_hot = (slot_list[:, None] == jnp.arange(group_tokens, dtype=jnp.int32)[None, :]).astype(jnp.bfloat16)
    token_sum = fold_slots(one_hot, per_expert.reshape(expert_total * per_source, local_width))
    return token_sum.astype(jnp.bfloat16)


def solution(mesh):
    expert_count, hidden_count = mesh.devices.shape
    split_mesh = Mesh(mesh.devices.reshape(expert_count, hidden_count // 2, 2), ("expert", "chip", "core"))
    in_specs = (
        P("expert", HIDDEN),
        P("expert", HIDDEN),
        P("expert", None, HIDDEN),
        P("expert", None, HIDDEN),
        P("expert", HIDDEN, None),
        P(None, "expert"),
        P(None, "expert"),
        P("expert", None, HIDDEN),
    )
    out_specs = P("expert", HIDDEN)
    return jax.shard_map(body, mesh=split_mesh, in_specs=in_specs, out_specs=out_specs, check_vma=False)
```

```python
import jax
import jax.numpy as jnp
from jax import lax
from jax.sharding import Mesh
from jax.sharding import PartitionSpec as P

keep_rate = 0.9
CROSS = ("expert", "chip")
HIDDEN = ("chip", "core")


def gelu_tanh(values):
    return jax.nn.gelu(values, approximate=True)


def fold_slots(one_hot, slot_values):
    high_part = slot_values.astype(jnp.bfloat16)
    low_part = (slot_values - high_part.astype(jnp.float32)).astype(jnp.bfloat16)
    dims = (((0,), (0,)), ((), ()))
    return lax.dot_general(one_hot, high_part, dims, preferred_element_type=jnp.float32) + lax.dot_general(
        one_hot, low_part, dims, preferred_element_type=jnp.float32
    )


def order_by_core(own, other, axis):
    first = lax.axis_index("core") == 0
    low = jnp.where(first, own, other)
    high = jnp.where(first, other, own)
    return jnp.stack([low, high], axis=axis)


def swap_cores(values):
    return lax.ppermute(values, "core", [(0, 1), (1, 0)])


def body(tokens, cotangent, w_gate, w_up, w_down, slot_token, slot_weight, keep_mask):
    gate_mat = w_gate[0]
    up_mat = w_up[0]
    down_mat = w_down[0]
    model_width, local_ff = gate_mat.shape
    chip_count = lax.axis_size("chip")
    expert_count = lax.axis_size("expert")
    expert_total, per_source = slot_token.shape
    slot_count = expert_count * per_source
    group_tokens, local_width = tokens.shape
    slot_list = slot_token.reshape(-1)
    weight_column = slot_weight.reshape(-1, 1)
    inv_keep = 1.0 / keep_rate

    one_hot = (slot_list[:, None] == jnp.arange(group_tokens, dtype=jnp.int32)[None, :]).astype(jnp.bfloat16)
    rows = jnp.dot(
        one_hot, jnp.concatenate([tokens, cotangent], axis=1), preferred_element_type=jnp.float32
    )
    chosen = rows[:, :local_width].astype(jnp.bfloat16)
    scaled = (weight_column * rows[:, local_width:]).astype(jnp.bfloat16)
    slab = jnp.concatenate([chosen, scaled], axis=1).reshape(expert_total, 1, per_source, 2 * local_width)
    outgoing = jnp.broadcast_to(slab, (expert_total, chip_count, per_source, 2 * local_width))
    outgoing = outgoing.reshape(expert_total * chip_count, per_source, 2 * local_width)
    own = lax.all_to_all(outgoing, CROSS, split_axis=0, concat_axis=0, tiled=True)
    own = own.reshape(expert_count, chip_count, per_source, 2 * local_width)
    other = swap_cores(own)
    full = order_by_core(own, other, axis=2)
    part_inputs = full[..., :local_width]
    part_cot = full[..., local_width:]

    gate_rows = gate_mat.reshape(chip_count, 2, local_width, local_ff)
    up_rows = up_mat.reshape(chip_count, 2, local_width, local_ff)
    down_cols = down_mat.reshape(local_ff, chip_count, 2, local_width)
    fwd_dims = (((1, 2, 4), (0, 1, 2)), ((), ()))
    gate_pre = lax.dot_general(part_inputs, gate_rows, fwd_dims, preferred_element_type=jnp.float32)
    up_pre = lax.dot_general(part_inputs, up_rows, fwd_dims, preferred_element_type=jnp.float32)
    grad_hidden = lax.dot_general(
        part_cot, down_cols, (((1, 2, 4), (1, 2, 3)), ((), ())), preferred_element_type=jnp.float32
    )
    gate_pre = gate_pre.reshape(slot_count, local_ff)
    up_pre = up_pre.reshape(slot_count, local_ff)
    grad_hidden = grad_hidden.reshape(slot_count, local_ff)
    activated, pullback = jax.vjp(gelu_tanh, gate_pre)
    grad_pre = grad_hidden * keep_mask[0].astype(jnp.float32) * inv_keep
    grad_up = (grad_pre * activated).astype(jnp.bfloat16)
    grad_gate = pullback(grad_pre * up_pre)[0].astype(jnp.bfloat16)
    grad_gate, grad_up = lax.optimization_barrier((grad_gate, grad_up))

    back_dims = (((1,), (1,)), ((), ()))
    partial = lax.dot_general(
        grad_gate, gate_mat, back_dims, preferred_element_type=jnp.float32
    ) + lax.dot_general(grad_up, up_mat, back_dims, preferred_element_type=jnp.float32)
    partial = partial.astype(jnp.bfloat16).reshape(expert_count, per_source, chip_count, 2, local_width)
    first = lax.axis_index("core") == 0
    keep_half = jnp.where(first, partial[:, :, :, 0], partial[:, :, :, 1])
    send_half = jnp.where(first, partial[:, :, :, 1], partial[:, :, :, 0])
    chip_sum = keep_half.astype(jnp.float32) + swap_cores(send_half).astype(jnp.float32)
    blocks = chip_sum.astype(jnp.bfloat16).transpose(0, 2, 1, 3)
    blocks = blocks.reshape(expert_count * chip_count, per_source, local_width)
    returned = lax.all_to_all(blocks, CROSS, split_axis=0, concat_axis=0, tiled=True)
    per_expert = returned.reshape(expert_total, chip_count, per_source, local_width).astype(jnp.float32).sum(1)
    token_sum = fold_slots(one_hot, per_expert.reshape(expert_total * per_source, local_width))
    return token_sum.astype(jnp.bfloat16)


def solution(mesh):
    expert_count, hidden_count = mesh.devices.shape
    split_mesh = Mesh(mesh.devices.reshape(expert_count, hidden_count // 2, 2), ("expert", "chip", "core"))
    in_specs = (
        P("expert", HIDDEN),
        P("expert", HIDDEN),
        P("expert", None, HIDDEN),
        P("expert", None, HIDDEN),
        P("expert", HIDDEN, None),
        P(None, "expert"),
        P(None, "expert"),
        P("expert", None, HIDDEN),
    )
    out_specs = P("expert", HIDDEN)
    return jax.shard_map(body, mesh=split_mesh, in_specs=in_specs, out_specs=out_specs, check_vma=False)
```

```python
import jax
import jax.numpy as jnp
from jax import lax
from jax.sharding import Mesh
from jax.sharding import PartitionSpec as P

keep_rate = 0.9
CROSS = ("expert", "chip")
HIDDEN = ("chip", "core")


def gelu_tanh(values):
    return jax.nn.gelu(values, approximate=True)


def fold_slots(one_hot, slot_values):
    high_part = slot_values.astype(jnp.bfloat16)
    low_part = (slot_values - high_part.astype(jnp.float32)).astype(jnp.bfloat16)
    dims = (((0,), (0,)), ((), ()))
    return lax.dot_general(one_hot, high_part, dims, preferred_element_type=jnp.float32) + lax.dot_general(
        one_hot, low_part, dims, preferred_element_type=jnp.float32
    )


def order_by_core(own, other, axis):
    first = lax.axis_index("core") == 0
    low = jnp.where(first, own, other)
    high = jnp.where(first, other, own)
    return jnp.stack([low, high], axis=axis)


def swap_cores(values):
    return lax.ppermute(values, "core", [(0, 1), (1, 0)])


def body(tokens, cotangent, w_gate, w_up, w_down, slot_token, slot_weight, keep_mask):
    gate_mat = w_gate[0]
    up_mat = w_up[0]
    down_mat = w_down[0]
    model_width, local_ff = gate_mat.shape
    chip_count = lax.axis_size("chip")
    expert_count = lax.axis_size("expert")
    expert_total, per_source = slot_token.shape
    slot_count = expert_count * per_source
    group_tokens, local_width = tokens.shape
    slot_list = slot_token.reshape(-1)
    weight_column = slot_weight.reshape(-1, 1)
    inv_keep = 1.0 / keep_rate

    one_hot = (slot_list[:, None] == jnp.arange(group_tokens, dtype=jnp.int32)[None, :]).astype(jnp.bfloat16)
    rows = jnp.dot(
        one_hot, jnp.concatenate([tokens, cotangent], axis=1), preferred_element_type=jnp.float32
    )
    chosen = rows[:, :local_width].astype(jnp.bfloat16)
    scaled = (weight_column * rows[:, local_width:]).astype(jnp.bfloat16)
    slab = jnp.concatenate([chosen, scaled], axis=1).reshape(expert_total, 1, per_source, 2 * local_width)
    outgoing = jnp.broadcast_to(slab, (expert_total, chip_count, per_source, 2 * local_width))
    outgoing = outgoing.reshape(expert_total * chip_count, per_source, 2 * local_width)
    own = lax.all_to_all(outgoing, CROSS, split_axis=0, concat_axis=0, tiled=True)
    own = own.reshape(expert_count, chip_count, per_source, 2 * local_width)
    other = swap_cores(own)
    full = order_by_core(own, other, axis=2)
    part_inputs = full[..., :local_width]
    part_cot = full[..., local_width:].transpose(0, 3, 1, 2, 4).reshape(slot_count, model_width)

    gate_rows = gate_mat.reshape(chip_count, 2, local_width, local_ff)
    up_rows = up_mat.reshape(chip_count, 2, local_width, local_ff)
    fwd_dims = (((1, 2, 4), (0, 1, 2)), ((), ()))
    gate_pre = lax.dot_general(part_inputs, gate_rows, fwd_dims, preferred_element_type=jnp.float32)
    up_pre = lax.dot_general(part_inputs, up_rows, fwd_dims, preferred_element_type=jnp.float32)
    chunk = 1024 if model_width % 1024 == 0 else model_width
    grad_hidden = None
    for start in range(0, model_width, chunk):
        piece = lax.dot_general(
            part_cot[:, start:start + chunk],
            down_mat[:, start:start + chunk],
            (((1,), (1,)), ((), ())),
            preferred_element_type=jnp.float32,
        )
        grad_hidden = piece if grad_hidden is None else grad_hidden + piece
    gate_pre = gate_pre.reshape(slot_count, local_ff)
    up_pre = up_pre.reshape(slot_count, local_ff)
    activated, pullback = jax.vjp(gelu_tanh, gate_pre)
    grad_pre = grad_hidden * keep_mask[0].astype(jnp.float32) * inv_keep
    grad_up = (grad_pre * activated).astype(jnp.bfloat16)
    grad_gate = pullback(grad_pre * up_pre)[0].astype(jnp.bfloat16)
    grad_gate, grad_up = lax.optimization_barrier((grad_gate, grad_up))

    back_dims = (((1,), (1,)), ((), ()))
    partial = lax.dot_general(
        grad_gate, gate_mat, back_dims, preferred_element_type=jnp.float32
    ) + lax.dot_general(grad_up, up_mat, back_dims, preferred_element_type=jnp.float32)
    partial = partial.astype(jnp.bfloat16).reshape(expert_count, per_source, chip_count, 2, local_width)
    first = lax.axis_index("core") == 0
    keep_half = jnp.where(first, partial[:, :, :, 0], partial[:, :, :, 1])
    send_half = jnp.where(first, partial[:, :, :, 1], partial[:, :, :, 0])
    chip_sum = keep_half.astype(jnp.float32) + swap_cores(send_half).astype(jnp.float32)
    blocks = chip_sum.astype(jnp.bfloat16).transpose(0, 2, 1, 3)
    blocks = blocks.reshape(expert_count * chip_count, per_source, local_width)
    returned = lax.all_to_all(blocks, CROSS, split_axis=0, concat_axis=0, tiled=True)
    per_expert = returned.reshape(expert_total, chip_count, per_source, local_width).astype(jnp.float32).sum(1)
    token_sum = fold_slots(one_hot, per_expert.reshape(expert_total * per_source, local_width))
    return token_sum.astype(jnp.bfloat16)


def solution(mesh):
    expert_count, hidden_count = mesh.devices.shape
    split_mesh = Mesh(mesh.devices.reshape(expert_count, hidden_count // 2, 2), ("expert", "chip", "core"))
    in_specs = (
        P("expert", HIDDEN),
        P("expert", HIDDEN),
        P("expert", None, HIDDEN),
        P("expert", None, HIDDEN),
        P("expert", HIDDEN, None),
        P(None, "expert"),
        P(None, "expert"),
        P("expert", None, HIDDEN),
    )
    out_specs = P("expert", HIDDEN)
    return jax.shard_map(body, mesh=split_mesh, in_specs=in_specs, out_specs=out_specs, check_vma=False)
```

```python
import jax
import jax.numpy as jnp
from jax import lax
from jax.sharding import Mesh
from jax.sharding import PartitionSpec as P

keep_rate = 0.9
CROSS = ("expert", "chip")
HIDDEN = ("chip", "core")


def gelu_tanh(values):
    return jax.nn.gelu(values, approximate=True)


def fold_slots(one_hot, slot_values):
    high_part = slot_values.astype(jnp.bfloat16)
    low_part = (slot_values - high_part.astype(jnp.float32)).astype(jnp.bfloat16)
    dims = (((0, 1), (0, 1)), ((), ()))
    return lax.dot_general(one_hot, high_part, dims, preferred_element_type=jnp.float32) + lax.dot_general(
        one_hot, low_part, dims, preferred_element_type=jnp.float32
    )


def order_by_core(own, other, axis):
    first = lax.axis_index("core") == 0
    low = jnp.where(first, own, other)
    high = jnp.where(first, other, own)
    return jnp.stack([low, high], axis=axis)


def swap_cores(values):
    return lax.ppermute(values, "core", [(0, 1), (1, 0)])


def body(tokens, cotangent, w_gate, w_up, w_down, slot_token, slot_weight, keep_mask):
    gate_mat = w_gate[0]
    up_mat = w_up[0]
    down_mat = w_down[0]
    model_width, local_ff = gate_mat.shape
    chip_count = lax.axis_size("chip")
    expert_count = lax.axis_size("expert")
    expert_total, per_source = slot_token.shape
    slot_count = expert_count * per_source
    group_tokens, local_width = tokens.shape
    slot_list = slot_token.reshape(-1)
    weight_column = slot_weight.reshape(-1, 1)
    inv_keep = 1.0 / keep_rate

    one_hot = (slot_list[:, None] == jnp.arange(group_tokens, dtype=jnp.int32)[None, :]).astype(jnp.bfloat16)
    rows = jnp.dot(
        one_hot, jnp.concatenate([tokens, cotangent], axis=1), preferred_element_type=jnp.float32
    )
    chosen = rows[:, :local_width].astype(jnp.bfloat16)
    scaled = (weight_column * rows[:, local_width:]).astype(jnp.bfloat16)
    slab = jnp.concatenate([chosen, scaled], axis=1).reshape(expert_total, 1, per_source, 2 * local_width)
    outgoing = jnp.broadcast_to(slab, (expert_total, chip_count, per_source, 2 * local_width))
    outgoing = outgoing.reshape(expert_total * chip_count, per_source, 2 * local_width)
    own = lax.all_to_all(outgoing, CROSS, split_axis=0, concat_axis=0, tiled=True)
    own = own.reshape(expert_count, chip_count, per_source, 2 * local_width)
    other = swap_cores(own)
    full = order_by_core(own, other, axis=2)
    part_inputs = full[..., :local_width]
    part_cot = full[..., local_width:]

    gate_rows = gate_mat.reshape(chip_count, 2, local_width, local_ff)
    up_rows = up_mat.reshape(chip_count, 2, local_width, local_ff)
    down_cols = down_mat.reshape(local_ff, chip_count, 2, local_width)
    fwd_dims = (((1, 2, 4), (0, 1, 2)), ((), ()))
    gate_pre = lax.dot_general(part_inputs, gate_rows, fwd_dims, preferred_element_type=jnp.float32)
    up_pre = lax.dot_general(part_inputs, up_rows, fwd_dims, preferred_element_type=jnp.float32)
    grad_hidden = lax.dot_general(
        part_cot, down_cols, (((1, 2, 4), (1, 2, 3)), ((), ())), preferred_element_type=jnp.float32
    )
    gate_pre = gate_pre.reshape(slot_count, local_ff)
    up_pre = up_pre.reshape(slot_count, local_ff)
    grad_hidden = grad_hidden.reshape(slot_count, local_ff)
    activated, pullback = jax.vjp(gelu_tanh, gate_pre)
    grad_pre = grad_hidden * keep_mask[0].astype(jnp.float32) * inv_keep
    grad_up = (grad_pre * activated).astype(jnp.bfloat16)
    grad_gate = pullback(grad_pre * up_pre)[0].astype(jnp.bfloat16)
    grad_gate, grad_up = lax.optimization_barrier((grad_gate, grad_up))

    back_dims = (((1,), (1,)), ((), ()))
    partial = lax.dot_general(
        grad_gate, gate_mat, back_dims, preferred_element_type=jnp.float32
    ) + lax.dot_general(grad_up, up_mat, back_dims, preferred_element_type=jnp.float32)
    half = per_source // 2
    partial = partial.astype(jnp.bfloat16).reshape(expert_count, 2, half, model_width)
    first = lax.axis_index("core") == 0
    keep_rows = jnp.where(first, partial[:, 0], partial[:, 1])
    send_rows = jnp.where(first, partial[:, 1], partial[:, 0])
    chip_sum = keep_rows.astype(jnp.float32) + swap_cores(send_rows).astype(jnp.float32)
    blocks = chip_sum.astype(jnp.bfloat16).reshape(expert_count, half, chip_count, 2 * local_width)
    blocks = blocks.transpose(0, 2, 1, 3).reshape(expert_count * chip_count, half, 2 * local_width)
    returned = lax.all_to_all(blocks, CROSS, split_axis=0, concat_axis=0, tiled=True)
    per_expert = returned.reshape(expert_total, chip_count, half, 2 * local_width).astype(jnp.float32).sum(1)
    row_hot = one_hot.reshape(expert_total, 2, half, group_tokens)
    own_hot = jnp.where(first, row_hot[:, 0], row_hot[:, 1])
    chip_tokens = fold_slots(own_hot, per_expert)
    keep_cols = jnp.where(first, chip_tokens[:, :local_width], chip_tokens[:, local_width:])
    send_cols = jnp.where(first, chip_tokens[:, local_width:], chip_tokens[:, :local_width])
    token_sum = keep_cols + swap_cores(send_cols)
    return token_sum.astype(jnp.bfloat16)


def solution(mesh):
    expert_count, hidden_count = mesh.devices.shape
    split_mesh = Mesh(mesh.devices.reshape(expert_count, hidden_count // 2, 2), ("expert", "chip", "core"))
    in_specs = (
        P("expert", HIDDEN),
        P("expert", HIDDEN),
        P("expert", None, HIDDEN),
        P("expert", None, HIDDEN),
        P("expert", HIDDEN, None),
        P(None, "expert"),
        P(None, "expert"),
        P("expert", None, HIDDEN),
    )
    out_specs = P("expert", HIDDEN)
    return jax.shard_map(body, mesh=split_mesh, in_specs=in_specs, out_specs=out_specs, check_vma=False)
```

```python
import jax
import jax.numpy as jnp
from jax import lax
from jax.sharding import Mesh
from jax.sharding import PartitionSpec as P

keep_rate = 0.9
CROSS = ("expert", "chip")
HIDDEN = ("chip", "core")


def gelu_tanh(values):
    return jax.nn.gelu(values, approximate=True)


def fold_slots(one_hot, slot_values):
    high_part = slot_values.astype(jnp.bfloat16)
    low_part = (slot_values - high_part.astype(jnp.float32)).astype(jnp.bfloat16)
    dims = (((0, 1), (0, 1)), ((), ()))
    return lax.dot_general(one_hot, high_part, dims, preferred_element_type=jnp.float32) + lax.dot_general(
        one_hot, low_part, dims, preferred_element_type=jnp.float32
    )


def order_by_core(own, other, axis):
    first = lax.axis_index("core") == 0
    low = jnp.where(first, own, other)
    high = jnp.where(first, other, own)
    return jnp.stack([low, high], axis=axis)


def swap_cores(values):
    return lax.ppermute(values, "core", [(0, 1), (1, 0)])


def body(tokens, cotangent, w_gate, w_up, w_down, slot_token, slot_weight, keep_mask):
    gate_mat = w_gate[0]
    up_mat = w_up[0]
    down_mat = w_down[0]
    model_width, local_ff = gate_mat.shape
    chip_count = lax.axis_size("chip")
    expert_count = lax.axis_size("expert")
    expert_total, per_source = slot_token.shape
    slot_count = expert_count * per_source
    group_tokens, local_width = tokens.shape
    slot_list = slot_token.reshape(-1)
    weight_column = slot_weight.reshape(-1, 1)
    inv_keep = 1.0 / keep_rate

    group = lax.axis_index("expert")
    shifts = range(1, expert_count)

    def from_groups(local, pick):
        pieces = [pick(local, group)]
        for shift in shifts:
            moved = pick(local, (group + shift) % expert_count)
            pieces.append(lax.ppermute(moved, "expert", [(i, (i + shift) % expert_count) for i in range(expert_count)]))
        return jnp.stack(pieces)

    info = jnp.stack([slot_token.astype(jnp.float32), slot_weight], axis=1)
    info_rel = from_groups(info, lambda values, row: values[row])
    info_abs = info_rel[(group - jnp.arange(expert_count)) % expert_count]
    mine_tokens = info_abs[:, 0].astype(jnp.int32)
    mine_weights = info_abs[:, 1].reshape(slot_count, 1, 1, 1)

    raw = jnp.concatenate([tokens, cotangent], axis=1)
    outgoing = jnp.broadcast_to(raw[None], (chip_count, group_tokens, 2 * local_width))
    in_plane = lax.all_to_all(outgoing, "chip", split_axis=0, concat_axis=0, tiled=True)
    own = from_groups(in_plane, lambda values, row: values)
    other = swap_cores(own)
    full = order_by_core(own, other, axis=2)
    block_rel = (group - jnp.arange(expert_count)) % expert_count
    column = (block_rel[:, None] * group_tokens + mine_tokens).reshape(-1)
    pick = (column[:, None] == jnp.arange(expert_count * group_tokens)[None, :]).astype(jnp.bfloat16)
    pick = pick.reshape(slot_count, expert_count, group_tokens)
    rows = lax.dot_general(pick, full, (((1, 2), (0, 3)), ((), ())), preferred_element_type=jnp.float32)
    part_inputs = rows[..., :local_width].astype(jnp.bfloat16)
    part_cot = (mine_weights * rows[..., local_width:]).astype(jnp.bfloat16)

    gate_rows = gate_mat.reshape(chip_count, 2, local_width, local_ff)
    up_rows = up_mat.reshape(chip_count, 2, local_width, local_ff)
    down_cols = down_mat.reshape(local_ff, chip_count, 2, local_width)
    fwd_dims = (((1, 2, 3), (0, 1, 2)), ((), ()))
    gate_pre = lax.dot_general(part_inputs, gate_rows, fwd_dims, preferred_element_type=jnp.float32)
    up_pre = lax.dot_general(part_inputs, up_rows, fwd_dims, preferred_element_type=jnp.float32)
    grad_hidden = lax.dot_general(
        part_cot, down_cols, (((1, 2, 3), (1, 2, 3)), ((), ())), preferred_element_type=jnp.float32
    )
    gate_pre = gate_pre.reshape(slot_count, local_ff)
    up_pre = up_pre.reshape(slot_count, local_ff)
    grad_hidden = grad_hidden.reshape(slot_count, local_ff)
    activated, pullback = jax.vjp(gelu_tanh, gate_pre)
    grad_pre = grad_hidden * keep_mask[0].astype(jnp.float32) * inv_keep
    grad_up = (grad_pre * activated).astype(jnp.bfloat16)
    grad_gate = pullback(grad_pre * up_pre)[0].astype(jnp.bfloat16)
    grad_gate, grad_up = lax.optimization_barrier((grad_gate, grad_up))

    back_dims = (((1,), (1,)), ((), ()))
    partial = lax.dot_general(
        grad_gate, gate_mat, back_dims, preferred_element_type=jnp.float32
    ) + lax.dot_general(grad_up, up_mat, back_dims, preferred_element_type=jnp.float32)
    half = per_source // 2
    partial = partial.astype(jnp.bfloat16).reshape(expert_count, 2, half, model_width)
    first = lax.axis_index("core") == 0
    keep_rows = jnp.where(first, partial[:, 0], partial[:, 1])
    send_rows = jnp.where(first, partial[:, 1], partial[:, 0])
    chip_sum = keep_rows.astype(jnp.float32) + swap_cores(send_rows).astype(jnp.float32)
    blocks = chip_sum.astype(jnp.bfloat16).reshape(expert_count, half, chip_count, 2 * local_width)
    blocks = blocks.transpose(0, 2, 1, 3).reshape(expert_count * chip_count, half, 2 * local_width)
    returned = lax.all_to_all(blocks, CROSS, split_axis=0, concat_axis=0, tiled=True)
    per_expert = returned.reshape(expert_total, chip_count, half, 2 * local_width).astype(jnp.float32).sum(1)
    one_hot = (slot_list[:, None] == jnp.arange(group_tokens, dtype=jnp.int32)[None, :]).astype(jnp.bfloat16)
    row_hot = one_hot.reshape(expert_total, 2, half, group_tokens)
    own_hot = jnp.where(first, row_hot[:, 0], row_hot[:, 1])
    chip_tokens = fold_slots(own_hot, per_expert)
    keep_cols = jnp.where(first, chip_tokens[:, :local_width], chip_tokens[:, local_width:])
    send_cols = jnp.where(first, chip_tokens[:, local_width:], chip_tokens[:, :local_width])
    token_sum = keep_cols + swap_cores(send_cols)
    return token_sum.astype(jnp.bfloat16)


def solution(mesh):
    expert_count, hidden_count = mesh.devices.shape
    split_mesh = Mesh(mesh.devices.reshape(expert_count, hidden_count // 2, 2), ("expert", "chip", "core"))
    in_specs = (
        P("expert", HIDDEN),
        P("expert", HIDDEN),
        P("expert", None, HIDDEN),
        P("expert", None, HIDDEN),
        P("expert", HIDDEN, None),
        P(None, "expert"),
        P(None, "expert"),
        P("expert", None, HIDDEN),
    )
    out_specs = P("expert", HIDDEN)
    return jax.shard_map(body, mesh=split_mesh, in_specs=in_specs, out_specs=out_specs, check_vma=False)
```

```python
import jax
import jax.numpy as jnp
from jax import lax
from jax.sharding import Mesh
from jax.sharding import PartitionSpec as P

keep_rate = 0.9
CROSS = ("expert", "chip")
HIDDEN = ("chip", "core")


def gelu_tanh(values):
    return jax.nn.gelu(values, approximate=True)


def fold_slots(one_hot, slot_values):
    high_part = slot_values.astype(jnp.bfloat16)
    low_part = (slot_values - high_part.astype(jnp.float32)).astype(jnp.bfloat16)
    dims = (((0, 1), (0, 1)), ((), ()))
    return lax.dot_general(one_hot, high_part, dims, preferred_element_type=jnp.float32) + lax.dot_general(
        one_hot, low_part, dims, preferred_element_type=jnp.float32
    )


def order_by_core(own, other, axis):
    first = lax.axis_index("core") == 0
    low = jnp.where(first, own, other)
    high = jnp.where(first, other, own)
    return jnp.stack([low, high], axis=axis)


def swap_cores(values):
    return lax.ppermute(values, "core", [(0, 1), (1, 0)])


def body(tokens, cotangent, w_gate, w_up, w_down, slot_token, slot_weight, keep_mask):
    gate_mat = w_gate[0]
    up_mat = w_up[0]
    down_mat = w_down[0]
    model_width, local_ff = gate_mat.shape
    chip_count = lax.axis_size("chip")
    expert_count = lax.axis_size("expert")
    expert_total, per_source = slot_token.shape
    slot_count = expert_count * per_source
    group_tokens, local_width = tokens.shape
    slot_list = slot_token.reshape(-1)
    weight_column = slot_weight.reshape(-1, 1)
    inv_keep = 1.0 / keep_rate

    group = lax.axis_index("expert")
    shifts = range(1, expert_count)

    def from_groups(local, pick):
        pieces = [pick(local, group)]
        for shift in shifts:
            moved = pick(local, (group + shift) % expert_count)
            pieces.append(lax.ppermute(moved, "expert", [(i, (i + shift) % expert_count) for i in range(expert_count)]))
        return jnp.stack(pieces)

    info = jnp.stack([slot_token.astype(jnp.float32), slot_weight], axis=1)
    info_rel = from_groups(info, lambda values, row: values[row])
    info_abs = info_rel[(group - jnp.arange(expert_count)) % expert_count]
    mine_tokens = info_abs[:, 0].astype(jnp.int32)
    mine_weights = info_abs[:, 1].reshape(slot_count, 1, 1, 1)

    raw = jnp.concatenate([tokens, cotangent], axis=1)
    outgoing = jnp.broadcast_to(raw[None], (chip_count, group_tokens, 2 * local_width))
    in_plane = lax.all_to_all(outgoing, "chip", split_axis=0, concat_axis=0, tiled=True)
    own = from_groups(in_plane, lambda values, row: values)
    down_t, own = lax.optimization_barrier((jnp.transpose(down_mat), own))
    other = swap_cores(own)
    full = order_by_core(own, other, axis=2)
    block_rel = (group - jnp.arange(expert_count)) % expert_count
    column = (block_rel[:, None] * group_tokens + mine_tokens).reshape(-1)
    pick = (column[:, None] == jnp.arange(expert_count * group_tokens)[None, :]).astype(jnp.bfloat16)
    pick = pick.reshape(slot_count, expert_count, group_tokens)
    rows = lax.dot_general(pick, full, (((1, 2), (0, 3)), ((), ())), preferred_element_type=jnp.float32)
    part_inputs = rows[..., :local_width].astype(jnp.bfloat16)
    part_cot = (mine_weights * rows[..., local_width:]).astype(jnp.bfloat16)

    gate_rows = gate_mat.reshape(chip_count, 2, local_width, local_ff)
    up_rows = up_mat.reshape(chip_count, 2, local_width, local_ff)
    down_rows = down_t.reshape(chip_count, 2, local_width, local_ff)
    fwd_dims = (((1, 2, 3), (0, 1, 2)), ((), ()))
    gate_pre = lax.dot_general(part_inputs, gate_rows, fwd_dims, preferred_element_type=jnp.float32)
    up_pre = lax.dot_general(part_inputs, up_rows, fwd_dims, preferred_element_type=jnp.float32)
    grad_hidden = lax.dot_general(part_cot, down_rows, fwd_dims, preferred_element_type=jnp.float32)
    gate_pre = gate_pre.reshape(slot_count, local_ff)
    up_pre = up_pre.reshape(slot_count, local_ff)
    grad_hidden = grad_hidden.reshape(slot_count, local_ff)
    activated, pullback = jax.vjp(gelu_tanh, gate_pre)
    grad_pre = grad_hidden * keep_mask[0].astype(jnp.float32) * inv_keep
    grad_up = (grad_pre * activated).astype(jnp.bfloat16)
    grad_gate = pullback(grad_pre * up_pre)[0].astype(jnp.bfloat16)
    grad_gate, grad_up = lax.optimization_barrier((grad_gate, grad_up))

    back_dims = (((1,), (1,)), ((), ()))
    partial = lax.dot_general(
        grad_gate, gate_mat, back_dims, preferred_element_type=jnp.float32
    ) + lax.dot_general(grad_up, up_mat, back_dims, preferred_element_type=jnp.float32)
    half = per_source // 2
    partial = partial.astype(jnp.bfloat16).reshape(expert_count, 2, half, model_width)
    first = lax.axis_index("core") == 0
    keep_rows = jnp.where(first, partial[:, 0], partial[:, 1])
    send_rows = jnp.where(first, partial[:, 1], partial[:, 0])
    chip_sum = keep_rows.astype(jnp.float32) + swap_cores(send_rows).astype(jnp.float32)
    blocks = chip_sum.astype(jnp.bfloat16).reshape(expert_count, half, chip_count, 2 * local_width)
    blocks = blocks.transpose(0, 2, 1, 3).reshape(expert_count * chip_count, half, 2 * local_width)
    returned = lax.all_to_all(blocks, CROSS, split_axis=0, concat_axis=0, tiled=True)
    per_expert = returned.reshape(expert_total, chip_count, half, 2 * local_width).astype(jnp.float32).sum(1)
    one_hot = (slot_list[:, None] == jnp.arange(group_tokens, dtype=jnp.int32)[None, :]).astype(jnp.bfloat16)
    row_hot = one_hot.reshape(expert_total, 2, half, group_tokens)
    own_hot = jnp.where(first, row_hot[:, 0], row_hot[:, 1])
    chip_tokens = fold_slots(own_hot, per_expert)
    keep_cols = jnp.where(first, chip_tokens[:, :local_width], chip_tokens[:, local_width:])
    send_cols = jnp.where(first, chip_tokens[:, local_width:], chip_tokens[:, :local_width])
    token_sum = keep_cols + swap_cores(send_cols)
    return token_sum.astype(jnp.bfloat16)


def solution(mesh):
    expert_count, hidden_count = mesh.devices.shape
    split_mesh = Mesh(mesh.devices.reshape(expert_count, hidden_count // 2, 2), ("expert", "chip", "core"))
    in_specs = (
        P("expert", HIDDEN),
        P("expert", HIDDEN),
        P("expert", None, HIDDEN),
        P("expert", None, HIDDEN),
        P("expert", HIDDEN, None),
        P(None, "expert"),
        P(None, "expert"),
        P("expert", None, HIDDEN),
    )
    out_specs = P("expert", HIDDEN)
    return jax.shard_map(body, mesh=split_mesh, in_specs=in_specs, out_specs=out_specs, check_vma=False)
```

```python
import jax
import jax.numpy as jnp
from jax import lax
from jax.sharding import Mesh
from jax.sharding import PartitionSpec as P

keep_rate = 0.9
CROSS = ("expert", "chip")
HIDDEN = ("chip", "core")


def gelu_tanh(values):
    return jax.nn.gelu(values, approximate=True)


def fold_slots(one_hot, slot_values):
    high_part = slot_values.astype(jnp.bfloat16)
    low_part = (slot_values - high_part.astype(jnp.float32)).astype(jnp.bfloat16)
    dims = (((0, 1), (0, 1)), ((), ()))
    return lax.dot_general(one_hot, high_part, dims, preferred_element_type=jnp.float32) + lax.dot_general(
        one_hot, low_part, dims, preferred_element_type=jnp.float32
    )


def order_by_core(own, other, axis):
    first = lax.axis_index("core") == 0
    low = jnp.where(first, own, other)
    high = jnp.where(first, other, own)
    return jnp.stack([low, high], axis=axis)


def swap_cores(values):
    return lax.ppermute(values, "core", [(0, 1), (1, 0)])


def body(tokens, cotangent, w_gate, w_up, w_down, slot_token, slot_weight, keep_mask):
    gate_mat = w_gate[0]
    up_mat = w_up[0]
    down_mat = w_down[0]
    model_width, local_ff = gate_mat.shape
    chip_count = lax.axis_size("chip")
    expert_count = lax.axis_size("expert")
    expert_total, per_source = slot_token.shape
    slot_count = expert_count * per_source
    group_tokens, local_width = tokens.shape
    slot_list = slot_token.reshape(-1)
    weight_column = slot_weight.reshape(-1, 1)
    inv_keep = 1.0 / keep_rate

    group = lax.axis_index("expert")
    shifts = range(1, expert_count)

    def from_groups(local, pick):
        pieces = [pick(local, group)]
        for shift in shifts:
            moved = pick(local, (group + shift) % expert_count)
            pieces.append(lax.ppermute(moved, "expert", [(i, (i + shift) % expert_count) for i in range(expert_count)]))
        return jnp.stack(pieces)

    info = jnp.stack([slot_token.astype(jnp.float32), slot_weight], axis=1)
    info_rel = from_groups(info, lambda values, row: values[row])

    raw = jnp.concatenate([tokens, cotangent], axis=1)
    outgoing = jnp.broadcast_to(raw[None], (chip_count, group_tokens, 2 * local_width))
    in_plane = lax.all_to_all(outgoing, "chip", split_axis=0, concat_axis=0, tiled=True)
    own = from_groups(in_plane, lambda values, row: values)
    down_t, own, info_rel = lax.optimization_barrier((jnp.transpose(down_mat), own, info_rel))
    info_abs = info_rel[(group - jnp.arange(expert_count)) % expert_count]
    mine_tokens = info_abs[:, 0].astype(jnp.int32)
    mine_weights = info_abs[:, 1].reshape(slot_count, 1, 1, 1)
    other = swap_cores(own)
    full = order_by_core(own, other, axis=2)
    block_rel = (group - jnp.arange(expert_count)) % expert_count
    column = (block_rel[:, None] * group_tokens + mine_tokens).reshape(-1)
    pick = (column[:, None] == jnp.arange(expert_count * group_tokens)[None, :]).astype(jnp.bfloat16)
    pick = pick.reshape(slot_count, expert_count, group_tokens)
    rows = lax.dot_general(pick, full, (((1, 2), (0, 3)), ((), ())), preferred_element_type=jnp.float32)
    part_inputs = rows[..., :local_width].astype(jnp.bfloat16)
    part_cot = (mine_weights * rows[..., local_width:]).astype(jnp.bfloat16)

    gate_rows = gate_mat.reshape(chip_count, 2, local_width, local_ff)
    up_rows = up_mat.reshape(chip_count, 2, local_width, local_ff)
    down_rows = down_t.reshape(chip_count, 2, local_width, local_ff)
    fwd_dims = (((1, 2, 3), (0, 1, 2)), ((), ()))
    gate_pre = lax.dot_general(part_inputs, gate_rows, fwd_dims, preferred_element_type=jnp.float32)
    up_pre = lax.dot_general(part_inputs, up_rows, fwd_dims, preferred_element_type=jnp.float32)
    grad_hidden = lax.dot_general(part_cot, down_rows, fwd_dims, preferred_element_type=jnp.float32)
    gate_pre = gate_pre.reshape(slot_count, local_ff)
    up_pre = up_pre.reshape(slot_count, local_ff)
    grad_hidden = grad_hidden.reshape(slot_count, local_ff)
    activated, pullback = jax.vjp(gelu_tanh, gate_pre)
    grad_pre = grad_hidden * keep_mask[0].astype(jnp.float32) * inv_keep
    grad_up = (grad_pre * activated).astype(jnp.bfloat16)
    grad_gate = pullback(grad_pre * up_pre)[0].astype(jnp.bfloat16)
    grad_gate, grad_up = lax.optimization_barrier((grad_gate, grad_up))

    back_dims = (((1,), (1,)), ((), ()))
    partial = lax.dot_general(
        grad_gate, gate_mat, back_dims, preferred_element_type=jnp.float32
    ) + lax.dot_general(grad_up, up_mat, back_dims, preferred_element_type=jnp.float32)
    half = per_source // 2
    partial = partial.astype(jnp.bfloat16).reshape(expert_count, 2, half, model_width)
    first = lax.axis_index("core") == 0
    keep_rows = jnp.where(first, partial[:, 0], partial[:, 1])
    send_rows = jnp.where(first, partial[:, 1], partial[:, 0])
    chip_sum = keep_rows.astype(jnp.float32) + swap_cores(send_rows).astype(jnp.float32)
    blocks = chip_sum.astype(jnp.bfloat16).reshape(expert_count, half, chip_count, 2 * local_width)
    blocks = blocks.transpose(0, 2, 1, 3).reshape(expert_count * chip_count, half, 2 * local_width)
    returned = lax.all_to_all(blocks, CROSS, split_axis=0, concat_axis=0, tiled=True)
    per_expert = returned.reshape(expert_total, chip_count, half, 2 * local_width).astype(jnp.float32).sum(1)
    one_hot = (slot_list[:, None] == jnp.arange(group_tokens, dtype=jnp.int32)[None, :]).astype(jnp.bfloat16)
    row_hot = one_hot.reshape(expert_total, 2, half, group_tokens)
    own_hot = jnp.where(first, row_hot[:, 0], row_hot[:, 1])
    chip_tokens = fold_slots(own_hot, per_expert)
    keep_cols = jnp.where(first, chip_tokens[:, :local_width], chip_tokens[:, local_width:])
    send_cols = jnp.where(first, chip_tokens[:, local_width:], chip_tokens[:, :local_width])
    token_sum = keep_cols + swap_cores(send_cols)
    return token_sum.astype(jnp.bfloat16)


def solution(mesh):
    expert_count, hidden_count = mesh.devices.shape
    split_mesh = Mesh(mesh.devices.reshape(expert_count, hidden_count // 2, 2), ("expert", "chip", "core"))
    in_specs = (
        P("expert", HIDDEN),
        P("expert", HIDDEN),
        P("expert", None, HIDDEN),
        P("expert", None, HIDDEN),
        P("expert", HIDDEN, None),
        P(None, "expert"),
        P(None, "expert"),
        P("expert", None, HIDDEN),
    )
    out_specs = P("expert", HIDDEN)
    return jax.shard_map(body, mesh=split_mesh, in_specs=in_specs, out_specs=out_specs, check_vma=False)
```

```python
import jax
import jax.numpy as jnp
from jax import lax
from jax.sharding import Mesh
from jax.sharding import PartitionSpec as P

keep_rate = 0.9
CROSS = ("expert", "chip")
HIDDEN = ("chip", "core")


def gelu_tanh(values):
    return jax.nn.gelu(values, approximate=True)


def fold_slots(one_hot, slot_values):
    high_part = slot_values.astype(jnp.bfloat16)
    low_part = (slot_values - high_part.astype(jnp.float32)).astype(jnp.bfloat16)
    dims = (((0, 1), (0, 1)), ((), ()))
    return lax.dot_general(one_hot, high_part, dims, preferred_element_type=jnp.float32) + lax.dot_general(
        one_hot, low_part, dims, preferred_element_type=jnp.float32
    )


def order_by_core(own, other, axis):
    first = lax.axis_index("core") == 0
    low = jnp.where(first, own, other)
    high = jnp.where(first, other, own)
    return jnp.stack([low, high], axis=axis)


def swap_cores(values):
    return lax.ppermute(values, "core", [(0, 1), (1, 0)])


def body(tokens, cotangent, w_gate, w_up, w_down, slot_token, slot_weight, keep_mask):
    gate_mat = w_gate[0]
    up_mat = w_up[0]
    down_mat = w_down[0]
    model_width, local_ff = gate_mat.shape
    chip_count = lax.axis_size("chip")
    expert_count = lax.axis_size("expert")
    expert_total, per_source = slot_token.shape
    slot_count = expert_count * per_source
    group_tokens, local_width = tokens.shape
    slot_list = slot_token.reshape(-1)
    weight_column = slot_weight.reshape(-1, 1)
    inv_keep = 1.0 / keep_rate

    group = lax.axis_index("expert")
    shifts = range(1, expert_count)

    def from_groups(local, pick):
        pieces = [pick(local, group)]
        for shift in shifts:
            moved = pick(local, (group + shift) % expert_count)
            pieces.append(lax.ppermute(moved, "expert", [(i, (i + shift) % expert_count) for i in range(expert_count)]))
        return jnp.stack(pieces)

    info = jnp.stack([slot_token.astype(jnp.float32), slot_weight], axis=1)
    info_rel = from_groups(info, lambda values, row: values[row])

    raw = jnp.concatenate([tokens, cotangent], axis=1)
    outgoing = jnp.broadcast_to(raw[None], (chip_count, group_tokens, 2 * local_width))
    in_plane = lax.all_to_all(outgoing, "chip", split_axis=0, concat_axis=0, tiled=True)
    partner_plane = swap_cores(in_plane)
    own = from_groups(in_plane, lambda values, row: values)
    down_t, own, info_rel, partner_plane = lax.optimization_barrier(
        (jnp.transpose(down_mat), own, info_rel, partner_plane)
    )
    info_abs = info_rel[(group - jnp.arange(expert_count)) % expert_count]
    mine_tokens = info_abs[:, 0].astype(jnp.int32)
    mine_weights = info_abs[:, 1].reshape(slot_count, 1, 1, 1)
    other = jnp.concatenate([partner_plane[None], swap_cores(own[1:])], axis=0)
    full = order_by_core(own, other, axis=2)
    block_rel = (group - jnp.arange(expert_count)) % expert_count
    column = (block_rel[:, None] * group_tokens + mine_tokens).reshape(-1)
    pick = (column[:, None] == jnp.arange(expert_count * group_tokens)[None, :]).astype(jnp.bfloat16)
    pick = pick.reshape(slot_count, expert_count, group_tokens)
    rows = lax.dot_general(pick, full, (((1, 2), (0, 3)), ((), ())), preferred_element_type=jnp.float32)
    part_inputs = rows[..., :local_width].astype(jnp.bfloat16)
    part_cot = (mine_weights * rows[..., local_width:]).astype(jnp.bfloat16)

    gate_rows = gate_mat.reshape(chip_count, 2, local_width, local_ff)
    up_rows = up_mat.reshape(chip_count, 2, local_width, local_ff)
    down_rows = down_t.reshape(chip_count, 2, local_width, local_ff)
    fwd_dims = (((1, 2, 3), (0, 1, 2)), ((), ()))
    gate_pre = lax.dot_general(part_inputs, gate_rows, fwd_dims, preferred_element_type=jnp.float32)
    up_pre = lax.dot_general(part_inputs, up_rows, fwd_dims, preferred_element_type=jnp.float32)
    grad_hidden = lax.dot_general(part_cot, down_rows, fwd_dims, preferred_element_type=jnp.float32)
    gate_pre = gate_pre.reshape(slot_count, local_ff)
    up_pre = up_pre.reshape(slot_count, local_ff)
    grad_hidden = grad_hidden.reshape(slot_count, local_ff)
    activated, pullback = jax.vjp(gelu_tanh, gate_pre)
    grad_pre = grad_hidden * keep_mask[0].astype(jnp.float32) * inv_keep
    grad_up = (grad_pre * activated).astype(jnp.bfloat16)
    grad_gate = pullback(grad_pre * up_pre)[0].astype(jnp.bfloat16)
    grad_gate, grad_up = lax.optimization_barrier((grad_gate, grad_up))

    back_dims = (((1,), (1,)), ((), ()))
    partial = lax.dot_general(
        grad_gate, gate_mat, back_dims, preferred_element_type=jnp.float32
    ) + lax.dot_general(grad_up, up_mat, back_dims, preferred_element_type=jnp.float32)
    half = per_source // 2
    partial = partial.astype(jnp.bfloat16).reshape(expert_count, 2, half, model_width)
    first = lax.axis_index("core") == 0
    keep_rows = jnp.where(first, partial[:, 0], partial[:, 1])
    send_rows = jnp.where(first, partial[:, 1], partial[:, 0])
    chip_sum = keep_rows.astype(jnp.float32) + swap_cores(send_rows).astype(jnp.float32)
    blocks = chip_sum.astype(jnp.bfloat16).reshape(expert_count, half, chip_count, 2 * local_width)
    blocks = blocks.transpose(0, 2, 1, 3).reshape(expert_count * chip_count, half, 2 * local_width)
    returned = lax.all_to_all(blocks, CROSS, split_axis=0, concat_axis=0, tiled=True)
    per_expert = returned.reshape(expert_total, chip_count, half, 2 * local_width).astype(jnp.float32).sum(1)
    one_hot = (slot_list[:, None] == jnp.arange(group_tokens, dtype=jnp.int32)[None, :]).astype(jnp.bfloat16)
    row_hot = one_hot.reshape(expert_total, 2, half, group_tokens)
    own_hot = jnp.where(first, row_hot[:, 0], row_hot[:, 1])
    chip_tokens = fold_slots(own_hot, per_expert)
    keep_cols = jnp.where(first, chip_tokens[:, :local_width], chip_tokens[:, local_width:])
    send_cols = jnp.where(first, chip_tokens[:, local_width:], chip_tokens[:, :local_width])
    token_sum = keep_cols + swap_cores(send_cols)
    return token_sum.astype(jnp.bfloat16)


def solution(mesh):
    expert_count, hidden_count = mesh.devices.shape
    split_mesh = Mesh(mesh.devices.reshape(expert_count, hidden_count // 2, 2), ("expert", "chip", "core"))
    in_specs = (
        P("expert", HIDDEN),
        P("expert", HIDDEN),
        P("expert", None, HIDDEN),
        P("expert", None, HIDDEN),
        P("expert", HIDDEN, None),
        P(None, "expert"),
        P(None, "expert"),
        P("expert", None, HIDDEN),
    )
    out_specs = P("expert", HIDDEN)
    return jax.shard_map(body, mesh=split_mesh, in_specs=in_specs, out_specs=out_specs, check_vma=False)
```

```python
import jax
import jax.numpy as jnp
from jax import lax
from jax.sharding import Mesh
from jax.sharding import PartitionSpec as P

keep_rate = 0.9
CROSS = ("expert", "chip")
HIDDEN = ("chip", "core")


def gelu_tanh(values):
    return jax.nn.gelu(values, approximate=True)


def fold_slots(one_hot, slot_values):
    high_part = slot_values.astype(jnp.bfloat16)
    low_part = (slot_values - high_part.astype(jnp.float32)).astype(jnp.bfloat16)
    dims = (((0, 1), (0, 1)), ((), ()))
    return lax.dot_general(one_hot, high_part, dims, preferred_element_type=jnp.float32) + lax.dot_general(
        one_hot, low_part, dims, preferred_element_type=jnp.float32
    )


def order_by_core(own, other, axis):
    first = lax.axis_index("core") == 0
    low = jnp.where(first, own, other)
    high = jnp.where(first, other, own)
    return jnp.stack([low, high], axis=axis)


def swap_cores(values):
    return lax.ppermute(values, "core", [(0, 1), (1, 0)])


def body(tokens, cotangent, w_gate, w_up, w_down, slot_token, slot_weight, keep_mask):
    gate_mat = w_gate[0]
    up_mat = w_up[0]
    down_mat = w_down[0]
    model_width, local_ff = gate_mat.shape
    chip_count = lax.axis_size("chip")
    expert_count = lax.axis_size("expert")
    expert_total, per_source = slot_token.shape
    slot_count = expert_count * per_source
    group_tokens, local_width = tokens.shape
    slot_list = slot_token.reshape(-1)
    weight_column = slot_weight.reshape(-1, 1)
    inv_keep = 1.0 / keep_rate

    group = lax.axis_index("expert")
    shifts = range(1, expert_count)

    def from_groups(local, pick):
        pieces = [pick(local, group)]
        for shift in shifts:
            moved = pick(local, (group + shift) % expert_count)
            pieces.append(lax.ppermute(moved, "expert", [(i, (i + shift) % expert_count) for i in range(expert_count)]))
        return jnp.stack(pieces)

    raw = jnp.concatenate([tokens, cotangent], axis=1)
    outgoing = jnp.broadcast_to(raw[None], (chip_count, group_tokens, 2 * local_width))
    in_plane = lax.all_to_all(outgoing, "chip", split_axis=0, concat_axis=0, tiled=True)
    partner_plane = swap_cores(in_plane)
    token_ids = jnp.arange(group_tokens, dtype=jnp.int32)

    def rows_for(plane, expert):
        pick = (slot_token[expert][:, None] == token_ids[None, :]).astype(jnp.bfloat16)
        picked = lax.dot_general(pick, plane, (((1,), (1,)), ((), ())), preferred_element_type=jnp.float32)
        scaled = slot_weight[expert].reshape(-1, 1, 1) * picked[..., local_width:]
        return jnp.concatenate(
            [picked[..., :local_width].astype(jnp.bfloat16), scaled.astype(jnp.bfloat16)], axis=-1
        )

    own_rel = [rows_for(in_plane, group)]
    partner_rel = [rows_for(partner_plane, group)]
    for shift in shifts:
        target = (group + shift) % expert_count
        perm = [(i, (i + shift) % expert_count) for i in range(expert_count)]
        moved = lax.ppermute(rows_for(in_plane, target), "expert", perm)
        own_rel.append(moved)
        partner_rel.append(swap_cores(moved))
    block_rel = (group - jnp.arange(expert_count)) % expert_count
    own = jnp.stack(own_rel)[block_rel]
    other = jnp.stack(partner_rel)[block_rel]
    down_t, own, other = lax.optimization_barrier((jnp.transpose(down_mat), own, other))
    full = order_by_core(own, other, axis=3).reshape(slot_count, chip_count, 2, 2 * local_width)
    part_inputs = full[..., :local_width]
    part_cot = full[..., local_width:]

    gate_rows = gate_mat.reshape(chip_count, 2, local_width, local_ff)
    up_rows = up_mat.reshape(chip_count, 2, local_width, local_ff)
    down_rows = down_t.reshape(chip_count, 2, local_width, local_ff)
    fwd_dims = (((1, 2, 3), (0, 1, 2)), ((), ()))
    gate_pre = lax.dot_general(part_inputs, gate_rows, fwd_dims, preferred_element_type=jnp.float32)
    up_pre = lax.dot_general(part_inputs, up_rows, fwd_dims, preferred_element_type=jnp.float32)
    grad_hidden = lax.dot_general(part_cot, down_rows, fwd_dims, preferred_element_type=jnp.float32)
    gate_pre = gate_pre.reshape(slot_count, local_ff)
    up_pre = up_pre.reshape(slot_count, local_ff)
    grad_hidden = grad_hidden.reshape(slot_count, local_ff)
    activated, pullback = jax.vjp(gelu_tanh, gate_pre)
    grad_pre = grad_hidden * keep_mask[0].astype(jnp.float32) * inv_keep
    grad_up = (grad_pre * activated).astype(jnp.bfloat16)
    grad_gate = pullback(grad_pre * up_pre)[0].astype(jnp.bfloat16)
    grad_gate, grad_up = lax.optimization_barrier((grad_gate, grad_up))

    back_dims = (((1,), (1,)), ((), ()))
    partial = lax.dot_general(
        grad_gate, gate_mat, back_dims, preferred_element_type=jnp.float32
    ) + lax.dot_general(grad_up, up_mat, back_dims, preferred_element_type=jnp.float32)
    half = per_source // 2
    partial = partial.astype(jnp.bfloat16).reshape(expert_count, 2, half, model_width)
    first = lax.axis_index("core") == 0
    keep_rows = jnp.where(first, partial[:, 0], partial[:, 1])
    send_rows = jnp.where(first, partial[:, 1], partial[:, 0])
    chip_sum = keep_rows.astype(jnp.float32) + swap_cores(send_rows).astype(jnp.float32)
    blocks = chip_sum.astype(jnp.bfloat16).reshape(expert_count, half, chip_count, 2 * local_width)
    blocks = blocks.transpose(0, 2, 1, 3).reshape(expert_count * chip_count, half, 2 * local_width)
    returned = lax.all_to_all(blocks, CROSS, split_axis=0, concat_axis=0, tiled=True)
    per_expert = returned.reshape(expert_total, chip_count, half, 2 * local_width).astype(jnp.float32).sum(1)
    one_hot = (slot_list[:, None] == jnp.arange(group_tokens, dtype=jnp.int32)[None, :]).astype(jnp.bfloat16)
    row_hot = one_hot.reshape(expert_total, 2, half, group_tokens)
    own_hot = jnp.where(first, row_hot[:, 0], row_hot[:, 1])
    chip_tokens = fold_slots(own_hot, per_expert)
    keep_cols = jnp.where(first, chip_tokens[:, :local_width], chip_tokens[:, local_width:])
    send_cols = jnp.where(first, chip_tokens[:, local_width:], chip_tokens[:, :local_width])
    token_sum = keep_cols + swap_cores(send_cols)
    return token_sum.astype(jnp.bfloat16)


def solution(mesh):
    expert_count, hidden_count = mesh.devices.shape
    split_mesh = Mesh(mesh.devices.reshape(expert_count, hidden_count // 2, 2), ("expert", "chip", "core"))
    in_specs = (
        P("expert", HIDDEN),
        P("expert", HIDDEN),
        P("expert", None, HIDDEN),
        P("expert", None, HIDDEN),
        P("expert", HIDDEN, None),
        P(None, "expert"),
        P(None, "expert"),
        P("expert", None, HIDDEN),
    )
    out_specs = P("expert", HIDDEN)
    return jax.shard_map(body, mesh=split_mesh, in_specs=in_specs, out_specs=out_specs, check_vma=False)
```

```python
import jax
import jax.numpy as jnp
from jax import lax
from jax.sharding import Mesh
from jax.sharding import PartitionSpec as P

keep_rate = 0.9
CROSS = ("expert", "chip")
HIDDEN = ("chip", "core")


def gelu_tanh(values):
    return jax.nn.gelu(values, approximate=True)


def fold_slots(one_hot, slot_values):
    high_part = slot_values.astype(jnp.bfloat16)
    low_part = (slot_values - high_part.astype(jnp.float32)).astype(jnp.bfloat16)
    dims = (((0, 1), (0, 1)), ((), ()))
    return lax.dot_general(one_hot, high_part, dims, preferred_element_type=jnp.float32) + lax.dot_general(
        one_hot, low_part, dims, preferred_element_type=jnp.float32
    )


def order_by_core(own, other, axis):
    first = lax.axis_index("core") == 0
    low = jnp.where(first, own, other)
    high = jnp.where(first, other, own)
    return jnp.stack([low, high], axis=axis)


def swap_cores(values):
    return lax.ppermute(values, "core", [(0, 1), (1, 0)])


def body(tokens, cotangent, w_gate, w_up, w_down, slot_token, slot_weight, keep_mask):
    gate_mat = w_gate[0]
    up_mat = w_up[0]
    down_mat = w_down[0]
    model_width, local_ff = gate_mat.shape
    chip_count = lax.axis_size("chip")
    expert_count = lax.axis_size("expert")
    expert_total, per_source = slot_token.shape
    slot_count = expert_count * per_source
    group_tokens, local_width = tokens.shape
    slot_list = slot_token.reshape(-1)
    weight_column = slot_weight.reshape(-1, 1)
    inv_keep = 1.0 / keep_rate

    group = lax.axis_index("expert")
    shifts = range(1, expert_count)

    def from_groups(local, pick):
        pieces = [pick(local, group)]
        for shift in shifts:
            moved = pick(local, (group + shift) % expert_count)
            pieces.append(lax.ppermute(moved, "expert", [(i, (i + shift) % expert_count) for i in range(expert_count)]))
        return jnp.stack(pieces)

    info = jnp.stack([slot_token.astype(jnp.float32), slot_weight], axis=1)
    info_rel = from_groups(info, lambda values, row: values[row])

    raw = jnp.concatenate([tokens, cotangent], axis=1)
    outgoing = jnp.broadcast_to(raw[None], (chip_count, group_tokens, 2 * local_width))
    outgoing, info_rel = lax.optimization_barrier((outgoing, info_rel))
    in_plane = lax.all_to_all(outgoing, "chip", split_axis=0, concat_axis=0, tiled=True)
    partner_plane = swap_cores(in_plane)
    own = from_groups(in_plane, lambda values, row: values)
    down_t, own, partner_plane = lax.optimization_barrier((jnp.transpose(down_mat), own, partner_plane))
    info_abs = info_rel[(group - jnp.arange(expert_count)) % expert_count]
    mine_tokens = info_abs[:, 0].astype(jnp.int32)
    mine_weights = info_abs[:, 1].reshape(slot_count, 1, 1, 1)
    other = jnp.concatenate([partner_plane[None], swap_cores(own[1:])], axis=0)
    full = order_by_core(own, other, axis=2)
    block_rel = (group - jnp.arange(expert_count)) % expert_count
    column = (block_rel[:, None] * group_tokens + mine_tokens).reshape(-1)
    pick = (column[:, None] == jnp.arange(expert_count * group_tokens)[None, :]).astype(jnp.bfloat16)
    pick = pick.reshape(slot_count, expert_count, group_tokens)
    rows = lax.dot_general(pick, full, (((1, 2), (0, 3)), ((), ())), preferred_element_type=jnp.float32)
    part_inputs = rows[..., :local_width].astype(jnp.bfloat16)
    part_cot = (mine_weights * rows[..., local_width:]).astype(jnp.bfloat16)

    gate_rows = gate_mat.reshape(chip_count, 2, local_width, local_ff)
    up_rows = up_mat.reshape(chip_count, 2, local_width, local_ff)
    down_rows = down_t.reshape(chip_count, 2, local_width, local_ff)
    fwd_dims = (((1, 2, 3), (0, 1, 2)), ((), ()))
    gate_pre = lax.dot_general(part_inputs, gate_rows, fwd_dims, preferred_element_type=jnp.float32)
    up_pre = lax.dot_general(part_inputs, up_rows, fwd_dims, preferred_element_type=jnp.float32)
    grad_hidden = lax.dot_general(part_cot, down_rows, fwd_dims, preferred_element_type=jnp.float32)
    gate_pre = gate_pre.reshape(slot_count, local_ff)
    up_pre = up_pre.reshape(slot_count, local_ff)
    grad_hidden = grad_hidden.reshape(slot_count, local_ff)
    activated, pullback = jax.vjp(gelu_tanh, gate_pre)
    grad_pre = grad_hidden * keep_mask[0].astype(jnp.float32) * inv_keep
    grad_up = (grad_pre * activated).astype(jnp.bfloat16)
    grad_gate = pullback(grad_pre * up_pre)[0].astype(jnp.bfloat16)
    grad_gate, grad_up = lax.optimization_barrier((grad_gate, grad_up))

    back_dims = (((1,), (1,)), ((), ()))
    partial = lax.dot_general(
        grad_gate, gate_mat, back_dims, preferred_element_type=jnp.float32
    ) + lax.dot_general(grad_up, up_mat, back_dims, preferred_element_type=jnp.float32)
    half = per_source // 2
    partial = partial.astype(jnp.bfloat16).reshape(expert_count, 2, half, model_width)
    first = lax.axis_index("core") == 0
    keep_rows = jnp.where(first, partial[:, 0], partial[:, 1])
    send_rows = jnp.where(first, partial[:, 1], partial[:, 0])
    chip_sum = keep_rows.astype(jnp.float32) + swap_cores(send_rows).astype(jnp.float32)
    blocks = chip_sum.astype(jnp.bfloat16).reshape(expert_count, half, chip_count, 2 * local_width)
    blocks = blocks.transpose(0, 2, 1, 3).reshape(expert_count * chip_count, half, 2 * local_width)
    returned = lax.all_to_all(blocks, CROSS, split_axis=0, concat_axis=0, tiled=True)
    per_expert = returned.reshape(expert_total, chip_count, half, 2 * local_width).astype(jnp.float32).sum(1)
    one_hot = (slot_list[:, None] == jnp.arange(group_tokens, dtype=jnp.int32)[None, :]).astype(jnp.bfloat16)
    row_hot = one_hot.reshape(expert_total, 2, half, group_tokens)
    own_hot = jnp.where(first, row_hot[:, 0], row_hot[:, 1])
    chip_tokens = fold_slots(own_hot, per_expert)
    keep_cols = jnp.where(first, chip_tokens[:, :local_width], chip_tokens[:, local_width:])
    send_cols = jnp.where(first, chip_tokens[:, local_width:], chip_tokens[:, :local_width])
    token_sum = keep_cols + swap_cores(send_cols)
    return token_sum.astype(jnp.bfloat16)


def solution(mesh):
    expert_count, hidden_count = mesh.devices.shape
    split_mesh = Mesh(mesh.devices.reshape(expert_count, hidden_count // 2, 2), ("expert", "chip", "core"))
    in_specs = (
        P("expert", HIDDEN),
        P("expert", HIDDEN),
        P("expert", None, HIDDEN),
        P("expert", None, HIDDEN),
        P("expert", HIDDEN, None),
        P(None, "expert"),
        P(None, "expert"),
        P("expert", None, HIDDEN),
    )
    out_specs = P("expert", HIDDEN)
    return jax.shard_map(body, mesh=split_mesh, in_specs=in_specs, out_specs=out_specs, check_vma=False)
```

```python
import jax
import jax.numpy as jnp
from jax import lax
from jax.sharding import Mesh
from jax.sharding import PartitionSpec as P

keep_rate = 0.9
CROSS = ("expert", "chip")
HIDDEN = ("chip", "core")


def gelu_tanh(values):
    return jax.nn.gelu(values, approximate=True)


def fold_slots(one_hot, slot_values):
    high_part = slot_values.astype(jnp.bfloat16)
    low_part = (slot_values - high_part.astype(jnp.float32)).astype(jnp.bfloat16)
    dims = (((0, 1), (0, 1)), ((), ()))
    return lax.dot_general(one_hot, high_part, dims, preferred_element_type=jnp.float32) + lax.dot_general(
        one_hot, low_part, dims, preferred_element_type=jnp.float32
    )


def order_by_core(own, other, axis):
    first = lax.axis_index("core") == 0
    low = jnp.where(first, own, other)
    high = jnp.where(first, other, own)
    return jnp.stack([low, high], axis=axis)


def swap_cores(values):
    return lax.ppermute(values, "core", [(0, 1), (1, 0)])


def body(tokens, cotangent, w_gate, w_up, w_down, slot_token, slot_weight, keep_mask):
    gate_mat = w_gate[0]
    up_mat = w_up[0]
    down_mat = w_down[0]
    model_width, local_ff = gate_mat.shape
    chip_count = lax.axis_size("chip")
    expert_count = lax.axis_size("expert")
    expert_total, per_source = slot_token.shape
    slot_count = expert_count * per_source
    group_tokens, local_width = tokens.shape
    slot_list = slot_token.reshape(-1)
    weight_column = slot_weight.reshape(-1, 1)
    inv_keep = 1.0 / keep_rate

    group = lax.axis_index("expert")
    shifts = range(1, expert_count)

    def from_groups(local, pick):
        pieces = [pick(local, group)]
        for shift in shifts:
            moved = pick(local, (group + shift) % expert_count)
            pieces.append(lax.ppermute(moved, "expert", [(i, (i + shift) % expert_count) for i in range(expert_count)]))
        return jnp.stack(pieces)

    info = jnp.stack([slot_token.astype(jnp.float32), slot_weight], axis=1)
    info_rel = from_groups(info, lambda values, row: values[row])

    raw = jnp.concatenate([tokens, cotangent], axis=1)
    outgoing = jnp.broadcast_to(raw[None], (chip_count, group_tokens, 2 * local_width))
    in_plane = lax.all_to_all(outgoing, "chip", split_axis=0, concat_axis=0, tiled=True)
    partner_plane = swap_cores(in_plane)
    own = from_groups(in_plane, lambda values, row: values)
    down_t, own, info_rel, partner_plane = lax.optimization_barrier(
        (jnp.transpose(down_mat), own, info_rel, partner_plane)
    )
    info_abs = info_rel[(group - jnp.arange(expert_count)) % expert_count]
    mine_tokens = info_abs[:, 0].astype(jnp.int32)
    mine_weights = info_abs[:, 1].reshape(slot_count, 1, 1, 1)
    other = jnp.concatenate([partner_plane[None], swap_cores(own[1:])], axis=0)
    full = lax.optimization_barrier(order_by_core(own, other, axis=2))
    block_rel = (group - jnp.arange(expert_count)) % expert_count
    column = (block_rel[:, None] * group_tokens + mine_tokens).reshape(-1)
    pick = (column[:, None] == jnp.arange(expert_count * group_tokens)[None, :]).astype(jnp.bfloat16)
    pick = pick.reshape(slot_count, expert_count, group_tokens)
    rows = lax.dot_general(pick, full, (((1, 2), (0, 3)), ((), ())), preferred_element_type=jnp.float32)
    part_inputs = rows[..., :local_width].astype(jnp.bfloat16)
    part_cot = (mine_weights * rows[..., local_width:]).astype(jnp.bfloat16)

    gate_rows = gate_mat.reshape(chip_count, 2, local_width, local_ff)
    up_rows = up_mat.reshape(chip_count, 2, local_width, local_ff)
    down_rows = down_t.reshape(chip_count, 2, local_width, local_ff)
    fwd_dims = (((1, 2, 3), (0, 1, 2)), ((), ()))
    gate_pre = lax.dot_general(part_inputs, gate_rows, fwd_dims, preferred_element_type=jnp.float32)
    up_pre = lax.dot_general(part_inputs, up_rows, fwd_dims, preferred_element_type=jnp.float32)
    grad_hidden = lax.dot_general(part_cot, down_rows, fwd_dims, preferred_element_type=jnp.float32)
    gate_pre = gate_pre.reshape(slot_count, local_ff)
    up_pre = up_pre.reshape(slot_count, local_ff)
    grad_hidden = grad_hidden.reshape(slot_count, local_ff)
    activated, pullback = jax.vjp(gelu_tanh, gate_pre)
    grad_pre = grad_hidden * keep_mask[0].astype(jnp.float32) * inv_keep
    grad_up = (grad_pre * activated).astype(jnp.bfloat16)
    grad_gate = pullback(grad_pre * up_pre)[0].astype(jnp.bfloat16)
    grad_gate, grad_up = lax.optimization_barrier((grad_gate, grad_up))

    back_dims = (((1,), (1,)), ((), ()))
    partial = lax.dot_general(
        grad_gate, gate_mat, back_dims, preferred_element_type=jnp.float32
    ) + lax.dot_general(grad_up, up_mat, back_dims, preferred_element_type=jnp.float32)
    half = per_source // 2
    partial = partial.astype(jnp.bfloat16).reshape(expert_count, 2, half, model_width)
    first = lax.axis_index("core") == 0
    keep_rows = jnp.where(first, partial[:, 0], partial[:, 1])
    send_rows = jnp.where(first, partial[:, 1], partial[:, 0])
    chip_sum = keep_rows.astype(jnp.float32) + swap_cores(send_rows).astype(jnp.float32)
    blocks = chip_sum.astype(jnp.bfloat16).reshape(expert_count, half, chip_count, 2 * local_width)
    blocks = blocks.transpose(0, 2, 1, 3).reshape(expert_count * chip_count, half, 2 * local_width)
    returned = lax.all_to_all(blocks, CROSS, split_axis=0, concat_axis=0, tiled=True)
    per_expert = returned.reshape(expert_total, chip_count, half, 2 * local_width).astype(jnp.float32).sum(1)
    one_hot = (slot_list[:, None] == jnp.arange(group_tokens, dtype=jnp.int32)[None, :]).astype(jnp.bfloat16)
    row_hot = one_hot.reshape(expert_total, 2, half, group_tokens)
    own_hot = jnp.where(first, row_hot[:, 0], row_hot[:, 1])
    chip_tokens = fold_slots(own_hot, per_expert)
    keep_cols = jnp.where(first, chip_tokens[:, :local_width], chip_tokens[:, local_width:])
    send_cols = jnp.where(first, chip_tokens[:, local_width:], chip_tokens[:, :local_width])
    token_sum = keep_cols + swap_cores(send_cols)
    return token_sum.astype(jnp.bfloat16)


def solution(mesh):
    expert_count, hidden_count = mesh.devices.shape
    split_mesh = Mesh(mesh.devices.reshape(expert_count, hidden_count // 2, 2), ("expert", "chip", "core"))
    in_specs = (
        P("expert", HIDDEN),
        P("expert", HIDDEN),
        P("expert", None, HIDDEN),
        P("expert", None, HIDDEN),
        P("expert", HIDDEN, None),
        P(None, "expert"),
        P(None, "expert"),
        P("expert", None, HIDDEN),
    )
    out_specs = P("expert", HIDDEN)
    return jax.shard_map(body, mesh=split_mesh, in_specs=in_specs, out_specs=out_specs, check_vma=False)
```

```python
import jax
import jax.numpy as jnp
from jax import lax
from jax.sharding import Mesh
from jax.sharding import PartitionSpec as P

keep_rate = 0.9
CROSS = ("expert", "chip")
HIDDEN = ("chip", "core")


def gelu_tanh(values):
    return jax.nn.gelu(values, approximate=True)


def fold_slots(one_hot, slot_values):
    high_part = slot_values.astype(jnp.bfloat16)
    low_part = (slot_values - high_part.astype(jnp.float32)).astype(jnp.bfloat16)
    dims = (((0, 1), (0, 1)), ((), ()))
    return lax.dot_general(one_hot, high_part, dims, preferred_element_type=jnp.float32) + lax.dot_general(
        one_hot, low_part, dims, preferred_element_type=jnp.float32
    )


def order_by_core(own, other, axis):
    first = lax.axis_index("core") == 0
    low = jnp.where(first, own, other)
    high = jnp.where(first, other, own)
    return jnp.stack([low, high], axis=axis)


def swap_cores(values):
    return lax.ppermute(values, "core", [(0, 1), (1, 0)])


def body(tokens, cotangent, w_gate, w_up, w_down, slot_token, slot_weight, keep_mask):
    gate_mat = w_gate[0]
    up_mat = w_up[0]
    down_mat = w_down[0]
    model_width, local_ff = gate_mat.shape
    chip_count = lax.axis_size("chip")
    expert_count = lax.axis_size("expert")
    expert_total, per_source = slot_token.shape
    slot_count = expert_count * per_source
    group_tokens, local_width = tokens.shape
    slot_list = slot_token.reshape(-1)
    weight_column = slot_weight.reshape(-1, 1)
    inv_keep = 1.0 / keep_rate

    group = lax.axis_index("expert")
    shifts = range(1, expert_count)

    def from_groups(local, pick):
        pieces = [pick(local, group)]
        for shift in shifts:
            moved = pick(local, (group + shift) % expert_count)
            pieces.append(lax.ppermute(moved, "expert", [(i, (i + shift) % expert_count) for i in range(expert_count)]))
        return jnp.stack(pieces)

    info = jnp.stack([slot_token.astype(jnp.float32), slot_weight], axis=1)
    info_rel = from_groups(info, lambda values, row: values[row])

    raw = jnp.concatenate([tokens, cotangent], axis=1)
    outgoing = jnp.broadcast_to(raw[None], (chip_count, group_tokens, 2 * local_width))
    in_plane = lax.all_to_all(outgoing, "chip", split_axis=0, concat_axis=0, tiled=True)
    in_plane, info_rel = lax.optimization_barrier((in_plane, info_rel))
    partner_plane = swap_cores(in_plane)
    own = from_groups(in_plane, lambda values, row: values)
    down_t, own, info_rel, partner_plane = lax.optimization_barrier(
        (jnp.transpose(down_mat), own, info_rel, partner_plane)
    )
    info_abs = info_rel[(group - jnp.arange(expert_count)) % expert_count]
    mine_tokens = info_abs[:, 0].astype(jnp.int32)
    mine_weights = info_abs[:, 1].reshape(slot_count, 1, 1, 1)
    other = jnp.concatenate([partner_plane[None], swap_cores(own[1:])], axis=0)
    full = lax.optimization_barrier(order_by_core(own, other, axis=2))
    block_rel = (group - jnp.arange(expert_count)) % expert_count
    column = (block_rel[:, None] * group_tokens + mine_tokens).reshape(-1)
    pick = (column[:, None] == jnp.arange(expert_count * group_tokens)[None, :]).astype(jnp.bfloat16)
    pick = pick.reshape(slot_count, expert_count, group_tokens)
    rows = lax.dot_general(pick, full, (((1, 2), (0, 3)), ((), ())), preferred_element_type=jnp.float32)
    part_inputs = rows[..., :local_width].astype(jnp.bfloat16)
    part_cot = (mine_weights * rows[..., local_width:]).astype(jnp.bfloat16)

    gate_rows = gate_mat.reshape(chip_count, 2, local_width, local_ff)
    up_rows = up_mat.reshape(chip_count, 2, local_width, local_ff)
    down_rows = down_t.reshape(chip_count, 2, local_width, local_ff)
    fwd_dims = (((1, 2, 3), (0, 1, 2)), ((), ()))
    gate_pre = lax.dot_general(part_inputs, gate_rows, fwd_dims, preferred_element_type=jnp.float32)
    up_pre = lax.dot_general(part_inputs, up_rows, fwd_dims, preferred_element_type=jnp.float32)
    grad_hidden = lax.dot_general(part_cot, down_rows, fwd_dims, preferred_element_type=jnp.float32)
    gate_pre = gate_pre.reshape(slot_count, local_ff)
    up_pre = up_pre.reshape(slot_count, local_ff)
    grad_hidden = grad_hidden.reshape(slot_count, local_ff)
    activated, pullback = jax.vjp(gelu_tanh, gate_pre)
    grad_pre = grad_hidden * keep_mask[0].astype(jnp.float32) * inv_keep
    grad_up = (grad_pre * activated).astype(jnp.bfloat16)
    grad_gate = pullback(grad_pre * up_pre)[0].astype(jnp.bfloat16)
    grad_gate, grad_up = lax.optimization_barrier((grad_gate, grad_up))

    back_dims = (((1,), (1,)), ((), ()))
    partial = lax.dot_general(
        grad_gate, gate_mat, back_dims, preferred_element_type=jnp.float32
    ) + lax.dot_general(grad_up, up_mat, back_dims, preferred_element_type=jnp.float32)
    half = per_source // 2
    partial = partial.astype(jnp.bfloat16).reshape(expert_count, 2, half, model_width)
    first = lax.axis_index("core") == 0
    keep_rows = jnp.where(first, partial[:, 0], partial[:, 1])
    send_rows = jnp.where(first, partial[:, 1], partial[:, 0])
    chip_sum = keep_rows.astype(jnp.float32) + swap_cores(send_rows).astype(jnp.float32)
    blocks = chip_sum.astype(jnp.bfloat16).reshape(expert_count, half, chip_count, 2 * local_width)
    blocks = blocks.transpose(0, 2, 1, 3).reshape(expert_count * chip_count, half, 2 * local_width)
    returned = lax.all_to_all(blocks, CROSS, split_axis=0, concat_axis=0, tiled=True)
    per_expert = returned.reshape(expert_total, chip_count, half, 2 * local_width).astype(jnp.float32).sum(1)
    one_hot = (slot_list[:, None] == jnp.arange(group_tokens, dtype=jnp.int32)[None, :]).astype(jnp.bfloat16)
    row_hot = one_hot.reshape(expert_total, 2, half, group_tokens)
    own_hot = jnp.where(first, row_hot[:, 0], row_hot[:, 1])
    chip_tokens = fold_slots(own_hot, per_expert)
    keep_cols = jnp.where(first, chip_tokens[:, :local_width], chip_tokens[:, local_width:])
    send_cols = jnp.where(first, chip_tokens[:, local_width:], chip_tokens[:, :local_width])
    token_sum = keep_cols + swap_cores(send_cols)
    return token_sum.astype(jnp.bfloat16)


def solution(mesh):
    expert_count, hidden_count = mesh.devices.shape
    split_mesh = Mesh(mesh.devices.reshape(expert_count, hidden_count // 2, 2), ("expert", "chip", "core"))
    in_specs = (
        P("expert", HIDDEN),
        P("expert", HIDDEN),
        P("expert", None, HIDDEN),
        P("expert", None, HIDDEN),
        P("expert", HIDDEN, None),
        P(None, "expert"),
        P(None, "expert"),
        P("expert", None, HIDDEN),
    )
    out_specs = P("expert", HIDDEN)
    return jax.shard_map(body, mesh=split_mesh, in_specs=in_specs, out_specs=out_specs, check_vma=False)
```

```python
import jax
import jax.numpy as jnp
from jax import lax
from jax.sharding import Mesh
from jax.sharding import PartitionSpec as P

keep_rate = 0.9
CROSS = ("expert", "chip")
HIDDEN = ("chip", "core")


def gelu_tanh(values):
    return jax.nn.gelu(values, approximate=True)


def fold_slots(one_hot, slot_values):
    high_part = slot_values.astype(jnp.bfloat16)
    low_part = (slot_values - high_part.astype(jnp.float32)).astype(jnp.bfloat16)
    dims = (((0, 1), (0, 1)), ((), ()))
    return lax.dot_general(one_hot, high_part, dims, preferred_element_type=jnp.float32) + lax.dot_general(
        one_hot, low_part, dims, preferred_element_type=jnp.float32
    )


def order_by_core(own, other, axis):
    first = lax.axis_index("core") == 0
    low = jnp.where(first, own, other)
    high = jnp.where(first, other, own)
    return jnp.stack([low, high], axis=axis)


def swap_cores(values):
    return lax.ppermute(values, "core", [(0, 1), (1, 0)])


def body(tokens, cotangent, w_gate, w_up, w_down, slot_token, slot_weight, keep_mask):
    gate_mat = w_gate[0]
    up_mat = w_up[0]
    down_mat = w_down[0]
    model_width, local_ff = gate_mat.shape
    chip_count = lax.axis_size("chip")
    expert_count = lax.axis_size("expert")
    expert_total, per_source = slot_token.shape
    slot_count = expert_count * per_source
    group_tokens, local_width = tokens.shape
    slot_list = slot_token.reshape(-1)
    weight_column = slot_weight.reshape(-1, 1)
    inv_keep = 1.0 / keep_rate

    group = lax.axis_index("expert")
    shifts = range(1, expert_count)

    def from_groups(local, pick):
        pieces = [pick(local, group)]
        for shift in shifts:
            moved = pick(local, (group + shift) % expert_count)
            pieces.append(lax.ppermute(moved, "expert", [(i, (i + shift) % expert_count) for i in range(expert_count)]))
        return jnp.stack(pieces)

    info = jnp.stack([slot_token.astype(jnp.float32), slot_weight], axis=1)
    info_rel = from_groups(info, lambda values, row: values[row])

    raw = jnp.concatenate([tokens, cotangent], axis=1)
    outgoing = jnp.broadcast_to(raw[None], (chip_count, group_tokens, 2 * local_width))
    in_plane = lax.all_to_all(outgoing, "chip", split_axis=0, concat_axis=0, tiled=True)
    partner_plane = swap_cores(in_plane)
    own = from_groups(in_plane, lambda values, row: values)
    down_t, own, info_rel, partner_plane = lax.optimization_barrier(
        (jnp.transpose(down_mat), own, info_rel, partner_plane)
    )
    info_abs = info_rel[(group - jnp.arange(expert_count)) % expert_count]
    mine_tokens = info_abs[:, 0].astype(jnp.int32)
    mine_weights = info_abs[:, 1].reshape(slot_count, 1, 1, 1)
    other = jnp.concatenate([partner_plane[None], swap_cores(own[1:])], axis=0)
    full = lax.optimization_barrier(order_by_core(own, other, axis=2))
    block_rel = (group - jnp.arange(expert_count)) % expert_count
    column = (block_rel[:, None] * group_tokens + mine_tokens).reshape(-1)
    pick = (column[:, None] == jnp.arange(expert_count * group_tokens)[None, :]).astype(jnp.bfloat16)
    pick = pick.reshape(slot_count, expert_count, group_tokens)
    rows = lax.dot_general(pick, full, (((1, 2), (0, 3)), ((), ())), preferred_element_type=jnp.float32)
    part_inputs = rows[..., :local_width].astype(jnp.bfloat16)
    part_cot = (mine_weights * rows[..., local_width:]).astype(jnp.bfloat16)

    gate_rows = gate_mat.reshape(chip_count, 2, local_width, local_ff)
    up_rows = up_mat.reshape(chip_count, 2, local_width, local_ff)
    down_rows = down_t.reshape(chip_count, 2, local_width, local_ff)
    fwd_dims = (((1, 2, 3), (0, 1, 2)), ((), ()))
    gate_pre = lax.dot_general(part_inputs, gate_rows, fwd_dims, preferred_element_type=jnp.float32)
    up_pre = lax.dot_general(part_inputs, up_rows, fwd_dims, preferred_element_type=jnp.float32)
    grad_hidden = lax.dot_general(part_cot, down_rows, fwd_dims, preferred_element_type=jnp.float32)
    gate_pre = gate_pre.reshape(slot_count, local_ff)
    up_pre = up_pre.reshape(slot_count, local_ff)
    grad_hidden = grad_hidden.reshape(slot_count, local_ff)
    activated, pullback = jax.vjp(gelu_tanh, gate_pre)
    grad_pre = grad_hidden * keep_mask[0].astype(jnp.float32) * inv_keep
    grad_up = (grad_pre * activated).astype(jnp.bfloat16)
    grad_gate = pullback(grad_pre * up_pre)[0].astype(jnp.bfloat16)
    grad_gate, grad_up = lax.optimization_barrier((grad_gate, grad_up))

    back_dims = (((1,), (1,)), ((), ()))
    partial = lax.dot_general(
        grad_gate, gate_mat, back_dims, preferred_element_type=jnp.float32
    ) + lax.dot_general(grad_up, up_mat, back_dims, preferred_element_type=jnp.float32)
    half = per_source // 2
    partial = partial.astype(jnp.bfloat16).reshape(expert_count, 2, half, chip_count, 2 * local_width)
    partial = partial.transpose(0, 1, 3, 2, 4)
    first = lax.axis_index("core") == 0
    keep_rows = jnp.where(first, partial[:, 0], partial[:, 1])
    send_rows = jnp.where(first, partial[:, 1], partial[:, 0])
    chip_sum = keep_rows.astype(jnp.float32) + swap_cores(send_rows).astype(jnp.float32)
    blocks = chip_sum.astype(jnp.bfloat16).reshape(expert_count * chip_count, half, 2 * local_width)
    returned = lax.all_to_all(blocks, CROSS, split_axis=0, concat_axis=0, tiled=True)
    per_expert = returned.reshape(expert_total, chip_count, half, 2 * local_width).astype(jnp.float32).sum(1)
    one_hot = (slot_list[:, None] == jnp.arange(group_tokens, dtype=jnp.int32)[None, :]).astype(jnp.bfloat16)
    row_hot = one_hot.reshape(expert_total, 2, half, group_tokens)
    own_hot = jnp.where(first, row_hot[:, 0], row_hot[:, 1])
    chip_tokens = fold_slots(own_hot, per_expert)
    keep_cols = jnp.where(first, chip_tokens[:, :local_width], chip_tokens[:, local_width:])
    send_cols = jnp.where(first, chip_tokens[:, local_width:], chip_tokens[:, :local_width])
    token_sum = keep_cols + swap_cores(send_cols)
    return token_sum.astype(jnp.bfloat16)


def solution(mesh):
    expert_count, hidden_count = mesh.devices.shape
    split_mesh = Mesh(mesh.devices.reshape(expert_count, hidden_count // 2, 2), ("expert", "chip", "core"))
    in_specs = (
        P("expert", HIDDEN),
        P("expert", HIDDEN),
        P("expert", None, HIDDEN),
        P("expert", None, HIDDEN),
        P("expert", HIDDEN, None),
        P(None, "expert"),
        P(None, "expert"),
        P("expert", None, HIDDEN),
    )
    out_specs = P("expert", HIDDEN)
    return jax.shard_map(body, mesh=split_mesh, in_specs=in_specs, out_specs=out_specs, check_vma=False)
```

```python
import jax
import jax.numpy as jnp
from jax import lax
from jax.sharding import Mesh
from jax.sharding import PartitionSpec as P

keep_rate = 0.9
CROSS = ("expert", "chip")
HIDDEN = ("chip", "core")


def gelu_tanh(values):
    return jax.nn.gelu(values, approximate=True)


def fold_slots(one_hot, slot_values):
    high_part = slot_values.astype(jnp.bfloat16)
    low_part = (slot_values - high_part.astype(jnp.float32)).astype(jnp.bfloat16)
    dims = (((0, 1), (0, 1)), ((), ()))
    return lax.dot_general(one_hot, high_part, dims, preferred_element_type=jnp.float32) + lax.dot_general(
        one_hot, low_part, dims, preferred_element_type=jnp.float32
    )


def order_by_core(own, other, axis):
    first = lax.axis_index("core") == 0
    low = jnp.where(first, own, other)
    high = jnp.where(first, other, own)
    return jnp.stack([low, high], axis=axis)


def swap_cores(values):
    return lax.ppermute(values, "core", [(0, 1), (1, 0)])


def body(tokens, cotangent, w_gate, w_up, w_down, slot_token, slot_weight, keep_mask):
    gate_mat = w_gate[0]
    up_mat = w_up[0]
    down_mat = w_down[0]
    model_width, local_ff = gate_mat.shape
    chip_count = lax.axis_size("chip")
    expert_count = lax.axis_size("expert")
    expert_total, per_source = slot_token.shape
    slot_count = expert_count * per_source
    group_tokens, local_width = tokens.shape
    slot_list = slot_token.reshape(-1)
    weight_column = slot_weight.reshape(-1, 1)
    inv_keep = 1.0 / keep_rate

    group = lax.axis_index("expert")
    shifts = range(1, expert_count)

    def from_groups(local, pick):
        pieces = [pick(local, group)]
        for shift in shifts:
            moved = pick(local, (group + shift) % expert_count)
            pieces.append(lax.ppermute(moved, "expert", [(i, (i + shift) % expert_count) for i in range(expert_count)]))
        return jnp.stack(pieces)

    info = jnp.stack([slot_token.astype(jnp.float32), slot_weight], axis=1)
    info_rel = from_groups(info, lambda values, row: values[row])

    raw = jnp.concatenate([tokens, cotangent], axis=1)
    outgoing = jnp.broadcast_to(raw[None], (chip_count, group_tokens, 2 * local_width))
    in_plane = lax.all_to_all(outgoing, "chip", split_axis=0, concat_axis=0, tiled=True)
    partner_plane = swap_cores(in_plane)
    own = from_groups(in_plane, lambda values, row: values)
    down_t, own, info_rel, partner_plane = lax.optimization_barrier(
        (jnp.transpose(down_mat), own, info_rel, partner_plane)
    )
    info_abs = info_rel[(group - jnp.arange(expert_count)) % expert_count]
    mine_tokens = info_abs[:, 0].astype(jnp.int32)
    mine_weights = info_abs[:, 1].reshape(slot_count, 1, 1, 1)
    other = jnp.concatenate([partner_plane[None], swap_cores(own[1:])], axis=0)
    full = lax.optimization_barrier(order_by_core(own, other, axis=2))
    block_rel = (group - jnp.arange(expert_count)) % expert_count
    column = (block_rel[:, None] * group_tokens + mine_tokens).reshape(-1)
    pick = (column[:, None] == jnp.arange(expert_count * group_tokens)[None, :]).astype(jnp.bfloat16)
    pick = pick.reshape(slot_count, expert_count, group_tokens)
    pick_dims = (((1, 2), (0, 3)), ((), ()))
    part_inputs = lax.dot_general(pick, full[..., :local_width], pick_dims, preferred_element_type=jnp.bfloat16)
    cot_rows = lax.dot_general(pick, full[..., local_width:], pick_dims, preferred_element_type=jnp.float32)
    part_cot = (mine_weights * cot_rows).astype(jnp.bfloat16)

    gate_rows = gate_mat.reshape(chip_count, 2, local_width, local_ff)
    up_rows = up_mat.reshape(chip_count, 2, local_width, local_ff)
    down_rows = down_t.reshape(chip_count, 2, local_width, local_ff)
    fwd_dims = (((1, 2, 3), (0, 1, 2)), ((), ()))
    gate_pre = lax.dot_general(part_inputs, gate_rows, fwd_dims, preferred_element_type=jnp.float32)
    up_pre = lax.dot_general(part_inputs, up_rows, fwd_dims, preferred_element_type=jnp.float32)
    grad_hidden = lax.dot_general(part_cot, down_rows, fwd_dims, preferred_element_type=jnp.float32)
    gate_pre = gate_pre.reshape(slot_count, local_ff)
    up_pre = up_pre.reshape(slot_count, local_ff)
    grad_hidden = grad_hidden.reshape(slot_count, local_ff)
    activated, pullback = jax.vjp(gelu_tanh, gate_pre)
    grad_pre = grad_hidden * keep_mask[0].astype(jnp.float32) * inv_keep
    grad_up = (grad_pre * activated).astype(jnp.bfloat16)
    grad_gate = pullback(grad_pre * up_pre)[0].astype(jnp.bfloat16)
    grad_gate, grad_up = lax.optimization_barrier((grad_gate, grad_up))

    back_dims = (((1,), (1,)), ((), ()))
    partial = lax.dot_general(
        grad_gate, gate_mat, back_dims, preferred_element_type=jnp.float32
    ) + lax.dot_general(grad_up, up_mat, back_dims, preferred_element_type=jnp.float32)
    half = per_source // 2
    partial = partial.astype(jnp.bfloat16).reshape(expert_count, 2, half, chip_count, 2 * local_width)
    partial = partial.transpose(0, 1, 3, 2, 4)
    first = lax.axis_index("core") == 0
    keep_rows = jnp.where(first, partial[:, 0], partial[:, 1])
    send_rows = jnp.where(first, partial[:, 1], partial[:, 0])
    chip_sum = keep_rows.astype(jnp.float32) + swap_cores(send_rows).astype(jnp.float32)
    blocks = chip_sum.astype(jnp.bfloat16).reshape(expert_count * chip_count, half, 2 * local_width)
    returned = lax.all_to_all(blocks, CROSS, split_axis=0, concat_axis=0, tiled=True)
    per_expert = returned.reshape(expert_total, chip_count, half, 2 * local_width).astype(jnp.float32).sum(1)
    one_hot = (slot_list[:, None] == jnp.arange(group_tokens, dtype=jnp.int32)[None, :]).astype(jnp.bfloat16)
    row_hot = one_hot.reshape(expert_total, 2, half, group_tokens)
    own_hot = jnp.where(first, row_hot[:, 0], row_hot[:, 1])
    chip_tokens = fold_slots(own_hot, per_expert)
    keep_cols = jnp.where(first, chip_tokens[:, :local_width], chip_tokens[:, local_width:])
    send_cols = jnp.where(first, chip_tokens[:, local_width:], chip_tokens[:, :local_width])
    token_sum = keep_cols + swap_cores(send_cols)
    return token_sum.astype(jnp.bfloat16)


def solution(mesh):
    expert_count, hidden_count = mesh.devices.shape
    split_mesh = Mesh(mesh.devices.reshape(expert_count, hidden_count // 2, 2), ("expert", "chip", "core"))
    in_specs = (
        P("expert", HIDDEN),
        P("expert", HIDDEN),
        P("expert", None, HIDDEN),
        P("expert", None, HIDDEN),
        P("expert", HIDDEN, None),
        P(None, "expert"),
        P(None, "expert"),
        P("expert", None, HIDDEN),
    )
    out_specs = P("expert", HIDDEN)
    return jax.shard_map(body, mesh=split_mesh, in_specs=in_specs, out_specs=out_specs, check_vma=False)
```

```python
import jax
import jax.numpy as jnp
from jax import lax
from jax.sharding import Mesh
from jax.sharding import PartitionSpec as P

keep_rate = 0.9
CROSS = ("expert", "chip")
HIDDEN = ("chip", "core")


def gelu_tanh(values):
    return jax.nn.gelu(values, approximate=True)


def fold_slots(one_hot, slot_values):
    high_part = slot_values.astype(jnp.bfloat16)
    low_part = (slot_values - high_part.astype(jnp.float32)).astype(jnp.bfloat16)
    dims = (((0, 1), (0, 1)), ((), ()))
    return lax.dot_general(one_hot, high_part, dims, preferred_element_type=jnp.float32) + lax.dot_general(
        one_hot, low_part, dims, preferred_element_type=jnp.float32
    )


def order_by_core(own, other, axis):
    first = lax.axis_index("core") == 0
    low = jnp.where(first, own, other)
    high = jnp.where(first, other, own)
    return jnp.stack([low, high], axis=axis)


def swap_cores(values):
    return lax.ppermute(values, "core", [(0, 1), (1, 0)])


def body(tokens, cotangent, w_gate, w_up, w_down, slot_token, slot_weight, keep_mask):
    gate_mat = w_gate[0]
    up_mat = w_up[0]
    down_mat = w_down[0]
    model_width, local_ff = gate_mat.shape
    chip_count = lax.axis_size("chip")
    expert_count = lax.axis_size("expert")
    expert_total, per_source = slot_token.shape
    slot_count = expert_count * per_source
    group_tokens, local_width = tokens.shape
    slot_list = slot_token.reshape(-1)
    weight_column = slot_weight.reshape(-1, 1)
    inv_keep = 1.0 / keep_rate

    group = lax.axis_index("expert")
    shifts = range(1, expert_count)

    def from_groups(local, pick):
        pieces = [pick(local, group)]
        for shift in shifts:
            moved = pick(local, (group + shift) % expert_count)
            pieces.append(lax.ppermute(moved, "expert", [(i, (i + shift) % expert_count) for i in range(expert_count)]))
        return jnp.stack(pieces)

    info = jnp.stack([slot_token.astype(jnp.float32), slot_weight], axis=1)
    info_rel = from_groups(info, lambda values, row: values[row])

    raw = jnp.concatenate([tokens, cotangent], axis=1)
    outgoing = jnp.broadcast_to(raw[None], (chip_count, group_tokens, 2 * local_width))
    in_plane = lax.all_to_all(outgoing, "chip", split_axis=0, concat_axis=0, tiled=True)
    partner_plane = swap_cores(in_plane)
    own = from_groups(in_plane, lambda values, row: values)
    down_t, own, info_rel, partner_plane = lax.optimization_barrier(
        (jnp.transpose(down_mat), own, info_rel, partner_plane)
    )
    info_abs = info_rel[(group - jnp.arange(expert_count)) % expert_count]
    mine_tokens = info_abs[:, 0].astype(jnp.int32)
    mine_weights = info_abs[:, 1].reshape(slot_count, 1, 1, 1)
    other = jnp.concatenate([partner_plane[None], swap_cores(own[1:])], axis=0)
    full = lax.optimization_barrier(order_by_core(own, other, axis=2))
    block_rel = (group - jnp.arange(expert_count)) % expert_count
    column = (block_rel[:, None] * group_tokens + mine_tokens).reshape(-1)
    pick = (column[:, None] == jnp.arange(expert_count * group_tokens)[None, :]).astype(jnp.bfloat16)
    pick = pick.reshape(slot_count, expert_count, group_tokens)
    rows = lax.dot_general(pick, full, (((1, 2), (0, 3)), ((), ())), preferred_element_type=jnp.float32)
    part_inputs = rows[..., :local_width].astype(jnp.bfloat16)
    part_cot = (mine_weights * rows[..., local_width:]).astype(jnp.bfloat16)

    gate_rows = gate_mat.reshape(chip_count, 2, local_width, local_ff)
    up_rows = up_mat.reshape(chip_count, 2, local_width, local_ff)
    down_rows = down_t.reshape(chip_count, 2, local_width, local_ff)
    fwd_dims = (((1, 2, 3), (0, 1, 2)), ((), ()))
    gate_pre = lax.dot_general(part_inputs, gate_rows, fwd_dims, preferred_element_type=jnp.float32)
    up_pre = lax.dot_general(part_inputs, up_rows, fwd_dims, preferred_element_type=jnp.float32)
    grad_hidden = lax.dot_general(part_cot, down_rows, fwd_dims, preferred_element_type=jnp.float32)
    gate_pre = gate_pre.reshape(slot_count, local_ff)
    up_pre = up_pre.reshape(slot_count, local_ff)
    grad_hidden = grad_hidden.reshape(slot_count, local_ff)
    activated, pullback = jax.vjp(gelu_tanh, gate_pre)
    grad_pre = grad_hidden * keep_mask[0].astype(jnp.float32) * inv_keep
    grad_up = (grad_pre * activated).astype(jnp.bfloat16)
    grad_gate = pullback(grad_pre * up_pre)[0].astype(jnp.bfloat16)
    grad_gate, grad_up = lax.optimization_barrier((grad_gate, grad_up))

    back_dims = (((1,), (1,)), ((), ()))
    partial = lax.dot_general(
        grad_gate, gate_mat, back_dims, preferred_element_type=jnp.float32
    ) + lax.dot_general(grad_up, up_mat, back_dims, preferred_element_type=jnp.float32)
    half = per_source // 2
    partial = partial.astype(jnp.bfloat16).reshape(expert_count, 2, half, chip_count, 2 * local_width)
    partial = partial.transpose(0, 1, 3, 2, 4)
    first = lax.axis_index("core") == 0
    keep_rows = jnp.where(first, partial[:, 0], partial[:, 1])
    send_rows = jnp.where(first, partial[:, 1], partial[:, 0])
    chip_sum = keep_rows.astype(jnp.float32) + swap_cores(send_rows).astype(jnp.float32)
    blocks = chip_sum.astype(jnp.bfloat16).reshape(expert_count * chip_count, half, 2 * local_width)
    returned = lax.all_to_all(blocks, CROSS, split_axis=0, concat_axis=0, tiled=True)
    per_expert = returned.reshape(expert_total, chip_count, half, 2 * local_width).astype(jnp.float32).sum(1)
    one_hot = (slot_list[:, None] == jnp.arange(group_tokens, dtype=jnp.int32)[None, :]).astype(jnp.bfloat16)
    row_hot = one_hot.reshape(expert_total, 2, half, group_tokens)
    own_hot = jnp.where(first, row_hot[:, 0], row_hot[:, 1])
    send_vals = jnp.where(first, per_expert[..., local_width:], per_expert[..., :local_width])
    keep_vals = jnp.where(first, per_expert[..., :local_width], per_expert[..., local_width:])
    swapped = swap_cores(fold_slots(own_hot, send_vals))
    token_sum = fold_slots(own_hot, keep_vals) + swapped
    return token_sum.astype(jnp.bfloat16)


def solution(mesh):
    expert_count, hidden_count = mesh.devices.shape
    split_mesh = Mesh(mesh.devices.reshape(expert_count, hidden_count // 2, 2), ("expert", "chip", "core"))
    in_specs = (
        P("expert", HIDDEN),
        P("expert", HIDDEN),
        P("expert", None, HIDDEN),
        P("expert", None, HIDDEN),
        P("expert", HIDDEN, None),
        P(None, "expert"),
        P(None, "expert"),
        P("expert", None, HIDDEN),
    )
    out_specs = P("expert", HIDDEN)
    return jax.shard_map(body, mesh=split_mesh, in_specs=in_specs, out_specs=out_specs, check_vma=False)
```
